512 devices in a mesh: chan: 16 (over x, y_lo, core), tile: 32 (over y_hi, z).
Axes of the slice: x: 4, y: 8 (y_hi: 4, y_lo: 2; y = y_hi * 2 + y_lo), z: 8, core: 2. Of those that a mesh axis runs over, the one named last changes fastest.
Arguments:
- channel_data: bfloat16 [16, 4096, 2048], P(None, 'tile', 'chan'), may hold values from -6 to 6
- delay_weights: bfloat16 [32, 16, 2048, 256], P('tile', None, 'chan'), may hold values from -0.046875 to 0.046875
- peak_lags: int32 [15, 128, 512], P(None, 'chan', 'tile'), may hold values from -15 to 15
- frame_pairs: int32 [15, 2], replicated, may hold values from 0 to 15, as said below
Outputs:
- quality: float32 [15, 128, 4096], P(None, 'chan', 'tile')
- strain: float32 [15, 128, 4096], P(None, 'chan', 'tile')
The draws below stay inside these ranges and needn't reach their ends.
Inputs may be any that keep to these rules, and one draw needn't show every extreme that they name: `frame_pairs`: the pairs follow one random order of all 16 frames: pair i holds its i-th and (i+1)-th frame, so the two frames of a pair differ and every frame occurs.
All inputs are finite; a program needn't handle non-finite values.
Results may differ from the reference program's by a relative error of at most 0.0003.
Values may be sent and summed in bfloat16 or wider, within the bound.
No kernel may reach another device: no remote copies, remote signals or barrier semaphores. Data moves between devices by JAX's collectives and lax.ppermute only.
A program may use at most 64 MiB of HBM per device.

```python
import jax
import jax.numpy as jnp
from jax import lax

CH = 1024
ZS = 128
FRAMES = 16
TAPS = 16
MAXLAG = 16
WIN = 32
BLK = 8
LINES = 128
TILES = 32
DEPTH = 4096
NPAIR = 15


def draw_frame_pairs(key, part):
    own_key = jax.random.fold_in(key, 7919)
    raw_scores = jax.random.randint(own_key, (FRAMES,), 0, 1 << 20, dtype=jnp.int32)
    distinct = raw_scores * FRAMES + jnp.arange(FRAMES, dtype=jnp.int32)
    ordering = jnp.argsort(distinct, stable=True).astype(jnp.int32)
    return jnp.stack([ordering[:-1], ordering[1:]], axis=1)


def with_ends(values, key, low, top_value):
    shape = values.shape
    place = [jax.random.randint(jax.random.fold_in(key, axis), (), 0, shape[axis]) for axis in range(len(shape))]
    values = values.at[tuple(place)].set(low)
    longest = shape.index(max(shape))
    place[longest] = (place[longest] + 1) % shape[longest]
    return values.at[tuple(place)].set(top_value)


def raised(drawn, rng, source, target, shards_of, factor):
    owner, partner = [(jnp.arange(drawn.shape[position]) // (drawn.shape[position] // shards_of)).reshape([-1 if axis == position else 1 for axis in range(drawn.ndim)]) for position in (source, target)]
    chosen = jax.random.permutation(rng, shards_of)[partner]
    strong = (owner == chosen) | (owner == (partner + shards_of // 2) % shards_of)
    return jnp.where(strong, factor * drawn, drawn)


def block_levels(key, extent, cuts, low, high):
    level = 1.0
    for axis_at, shards_of in cuts:
        steps = jax.random.uniform(jax.random.fold_in(jax.random.fold_in(key, 6), axis_at), (shards_of,), jnp.float32, low / len(cuts), high / len(cuts))
        level = level * jnp.repeat(jnp.exp(steps), extent[axis_at] // shards_of).reshape((-1,) + (1,) * (len(extent) - 1 - axis_at))
    return level


def centred(key, shape, spread, reach, split=(), held_as=jnp.bfloat16):
    result = jax.random.normal(key, shape, jnp.float32) * spread
    if len(split) > 0:
        result = block_levels(key, shape, split, -0.22, 0.18) * result
    return jnp.clip(result, min=-reach, max=reach).astype(held_as)


def gaussian_with(rng, shape, deviation, reach, split, heavy, held_as=jnp.bfloat16):
    values = deviation * jax.random.normal(rng, shape, jnp.float32)
    if split:
        values = values * block_levels(rng, shape, split, -0.22, 0.18)
    return jnp.clip(raised(values, jax.random.fold_in(rng, 3), *heavy), -reach, reach).astype(held_as)


def setup_inputs(seed: int = 0) -> dict:
    seeds = jax.random.split(jax.random.key(seed), 5)
    channel_data = centred(seeds[0], (FRAMES, DEPTH, 2 * CH), 1.0, 6.0, ((1, 32), (2, 16)))
    delay_weights = gaussian_with(seeds[1], (TILES, TAPS, 2 * CH, 2 * LINES), (TAPS * 2 * CH) ** -0.5, 0.046875, ((0, 32), (2, 16)), (2, 3, 16, 2.0))
    peak_lags = with_ends(jax.random.randint(seeds[2], (NPAIR, LINES, DEPTH // BLK), 1 - MAXLAG, MAXLAG), jax.random.fold_in(seeds[2], 1), 1 - MAXLAG, MAXLAG - 1).astype(jnp.int32)
    frame_pairs = draw_frame_pairs(jax.random.fold_in(seeds[4], 71), 0)
    return dict(channel_data=channel_data, delay_weights=delay_weights, peak_lags=peak_lags, frame_pairs=frame_pairs)


epsilon = 1e-05

def window_sum(values):
    dims = (1,) * (values.ndim - 1) + (WIN,)
    return lax.reduce_window(values, jnp.zeros((), values.dtype), lax.add, dims, (1,) * values.ndim, 'VALID')

def reference(channel_data, delay_weights, peak_lags, frame_pairs):
    padded = jnp.concatenate([channel_data.astype(jnp.float32), jnp.zeros((FRAMES, TAPS - 1, 2 * CH), jnp.float32)], axis=1)

    def beam_tile(tile_index):
        block_rows = lax.dynamic_slice_in_dim(padded, tile_index * ZS, ZS + TAPS - 1, 1)
        tile_weights = delay_weights[tile_index].astype(jnp.float32)
        summed = jnp.zeros((FRAMES, 2 * LINES, ZS), jnp.float32)
        for tap_index in range(TAPS):
            summed = summed + jnp.einsum('fzc,cm->fmz', block_rows[:, tap_index:tap_index + ZS], tile_weights[tap_index])
        return summed
    tiles_out = lax.map(beam_tile, jnp.arange(TILES, dtype=jnp.int32))
    volume = jnp.transpose(tiles_out, (1, 2, 0, 3)).reshape(FRAMES, 2 * LINES, DEPTH)
    halo_reach = MAXLAG + WIN // 2
    vol_padded = jnp.pad(volume, ((0, 0), (0, 0), (halo_reach, halo_reach)))
    span_len = DEPTH + WIN - 1
    lag_values = jnp.arange(-MAXLAG, MAXLAG + 1, dtype=jnp.int32)

    def pair_maps(pair_index):
        front = vol_padded[frame_pairs[pair_index, 0]].reshape(LINES, 2, -1)
        later_frame = vol_padded[frame_pairs[pair_index, 1]].reshape(LINES, 2, -1)
        first_part = front[:, :, MAXLAG:MAXLAG + span_len]
        power_a = window_sum(lax.optimization_barrier(jnp.sum(first_part * first_part, axis=1))) / (2 * WIN)

        def one_lag(shift_start):
            moved = lax.dynamic_slice_in_dim(later_frame, shift_start, span_len, 2)
            cross_sum = window_sum(lax.optimization_barrier(jnp.sum(first_part * moved, axis=1)))
            power_b = window_sum(lax.optimization_barrier(jnp.sum(moved * moved, axis=1))) / (2 * WIN)
            return cross_sum / (2 * WIN * jnp.sqrt(power_a + epsilon) * jnp.sqrt(power_b + epsilon))
        scores = lax.map(one_lag, jnp.arange(2 * MAXLAG + 1, dtype=jnp.int32))
        quality = lax.optimization_barrier(jnp.max(scores, axis=0))
        peak_full = jnp.repeat(peak_lags[pair_index], BLK, axis=1)

        def pick_lag(delta):
            return lax.optimization_barrier(jnp.sum(jnp.where(lag_values[:, None, None] == peak_full[None] + delta, scores, jnp.zeros_like(scores)), axis=0))
        at_prev = pick_lag(-1)
        centre = pick_lag(0)
        at_next = pick_lag(1)
        curvature = jnp.maximum(2.0 * centre - at_prev - at_next, 0.25)
        displacement = peak_full.astype(jnp.float32) + (at_next - at_prev) / (2.0 * curvature)
        disp_padded = jnp.pad(displacement, ((0, 0), (2, 2)))
        strain = (disp_padded[:, 0:DEPTH] - 8.0 * disp_padded[:, 1:DEPTH + 1] + 8.0 * disp_padded[:, 3:DEPTH + 3] - disp_padded[:, 4:DEPTH + 4]) / 12.0
        return (quality, strain)
    quality, strain = lax.map(pair_maps, jnp.arange(NPAIR, dtype=jnp.int32))
    return (quality, strain)
```

```python
import jax
import jax.numpy as jnp
from jax import lax
from jax.sharding import Mesh, PartitionSpec as P

MAXLAG = 16
WIN = 32
BLK = 8
HALO = MAXLAG + WIN // 2 + 2

epsilon = 1e-05

CHAN = ("cx", "cy", "cc")


def window_sum(values):
    width = 1
    while width < WIN:
        n = values.shape[-1] - width
        values = values[..., :n] + values[..., width : width + n]
        width *= 2
    return values


def from_left(block, axis):
    count = lax.axis_size(axis)
    return lax.ppermute(block, axis, [(i, i + 1) for i in range(count - 1)])


def from_right(block, axis):
    count = lax.axis_size(axis)
    return lax.ppermute(block, axis, [(i + 1, i) for i in range(count - 1)])


def beamform(extended, weights):
    return lax.conv_general_dilated(
        extended,
        weights,
        window_strides=(1,),
        padding="VALID",
        dimension_numbers=("NWC", "WIO", "NCW"),
        preferred_element_type=jnp.float32,
    )


def shards(channel_data, delay_weights, peak_lags, frame_pairs):
    frames, sample_rows, _ = channel_data.shape
    tap_count = delay_weights.shape[1]
    nx, ny, nc = (lax.axis_size(a) for a in CHAN)
    tile = lax.axis_index("tile")
    tiles = lax.axis_size("tile")

    lag_f = peak_lags.astype(jnp.float32)
    lag_prev = from_left(lag_f[:, :, -1:], "tile")
    lag_next = from_right(lag_f[:, :, :1], "tile")

    rim_rows = from_right(channel_data[:, : tap_count - 1, :], "tile")
    extended = jnp.concatenate([channel_data, rim_rows], axis=1)

    weights = delay_weights[0]
    taps, cin, cols = weights.shape
    per_dev = cols // (nx * ny * nc)
    w6 = weights.reshape(taps, cin, nx, ny, nc, per_dev)
    core = lax.axis_index("cc")
    w_mine = lax.dynamic_index_in_dim(w6, core, 4, keepdims=False).reshape(taps, cin, -1)
    w_other = lax.dynamic_index_in_dim(w6, 1 - core, 4, keepdims=False).reshape(taps, cin, -1)
    vol_other = beamform(extended, w_other)
    vol_mine = beamform(extended, w_mine)
    vol = vol_mine + lax.ppermute(vol_other, "cc", [(0, 1), (1, 0)])
    vol = vol.reshape(frames, nx * ny, per_dev, sample_rows)
    vol = lax.all_to_all(vol, ("cx", "cy"), 1, 1, tiled=True).sum(axis=1)

    head = vol[..., :HALO]
    tail = vol[..., sample_rows - HALO :]
    padded = jnp.concatenate([from_left(tail, "tile"), vol, from_right(head, "tile")], axis=2)

    line_count = per_dev // 2
    pair_count = frame_pairs.shape[0]
    front = padded[frame_pairs[:, 0]].reshape(pair_count, line_count, 2, -1)
    later = padded[frame_pairs[:, 1]].reshape(pair_count, line_count, 2, -1)
    out_len = sample_rows + 4
    prod_len = out_len + WIN - 1
    xr = front[:, :, 0, WIN // 2 : WIN // 2 + prod_len]
    xi = front[:, :, 1, WIN // 2 : WIN // 2 + prod_len]
    yr = later[:, :, 0]
    yi = later[:, :, 1]
    nlag = 2 * MAXLAG + 1
    prods = jnp.stack(
        [xr * yr[..., j : j + prod_len] + xi * yi[..., j : j + prod_len] for j in range(nlag)]
    )
    cross_sum = window_sum(prods)
    power_a = window_sum(xr * xr + xi * xi) / (2 * WIN)
    ey = yr * yr + yi * yi
    power_full = window_sum(ey[..., : out_len + nlag - 1 + WIN - 1]) / (2 * WIN)
    root_b = jnp.sqrt(power_full + epsilon)
    root_b = jnp.stack([root_b[..., j : j + out_len] for j in range(nlag)])
    scores = cross_sum / (2 * WIN * jnp.sqrt(power_a + epsilon)[None] * root_b)
    quality = jnp.max(scores[..., 2 : 2 + sample_rows], axis=0)

    own = jnp.repeat(lag_f, BLK, axis=2)
    peak_full = jnp.concatenate(
        [jnp.repeat(lag_prev, 2, axis=2), own, jnp.repeat(lag_next, 2, axis=2)], axis=2
    ).astype(jnp.int32)
    lag_values = jnp.arange(-MAXLAG, MAXLAG + 1, dtype=jnp.int32)[:, None, None, None]

    def pick_lag(delta):
        return jnp.sum(
            jnp.where(lag_values == peak_full[None] + delta, scores, jnp.zeros_like(scores)), axis=0
        )

    at_prev = pick_lag(-1)
    centre = pick_lag(0)
    at_next = pick_lag(1)
    curvature = jnp.maximum(2.0 * centre - at_prev - at_next, 0.25)
    displacement = peak_full.astype(jnp.float32) + (at_next - at_prev) / (2.0 * curvature)
    zo = lax.broadcasted_iota(jnp.int32, displacement.shape, 2)
    outside = ((tile == 0) & (zo < 2)) | ((tile == tiles - 1) & (zo >= sample_rows + 2))
    dz = jnp.where(outside, 0.0, displacement)
    strain = (
        dz[..., 0:sample_rows]
        - 8.0 * dz[..., 1 : sample_rows + 1]
        + 8.0 * dz[..., 3 : sample_rows + 3]
        - dz[..., 4 : sample_rows + 4]
    ) / 12.0
    return (quality, strain)


def solution(mesh):
    chan = mesh.shape["chan"]
    tile = mesh.shape["tile"]
    devices = mesh.devices.reshape(chan // 4, 2, 2, tile)
    fine = Mesh(devices, CHAN + ("tile",))
    return jax.shard_map(
        shards,
        mesh=fine,
        in_specs=(
            P(None, "tile", CHAN),
            P("tile", None, CHAN, None),
            P(None, CHAN, "tile"),
            P(),
        ),
        out_specs=(P(None, CHAN, "tile"), P(None, CHAN, "tile")),
        check_vma=False,
    )
```

```python
import jax
import jax.numpy as jnp
from jax import lax
from jax.experimental import pallas as pl
from jax.experimental.pallas import tpu as pltpu
from jax.sharding import Mesh, PartitionSpec as P

MAXLAG = 16
WIN = 32
BLK = 8
HALO = MAXLAG + WIN // 2 + 2
LANES = 256

epsilon = 1e-05

CHAN = ("cx", "cy", "cc")


def _wsum(a):
    width = 1
    while width < WIN:
        a = a + pltpu.roll(a, LANES - width, 1)
        width *= 2
    return a


def corr_kernel(fp_ref, v_ref, peak_ref, q_ref, d_ref):
    def pair(p, carry):
        fa = fp_ref[p, 0]
        fb = fp_ref[p, 1]
        xr = pltpu.roll(v_ref[fa, 0], LANES - WIN // 2, 1)
        xi = pltpu.roll(v_ref[fa, 1], LANES - WIN // 2, 1)
        yr = v_ref[fb, 0]
        yi = v_ref[fb, 1]
        root_a = jnp.sqrt(_wsum(xr * xr + xi * xi) / (2 * WIN) + epsilon)
        root_full = jnp.sqrt(_wsum(yr * yr + yi * yi) / (2 * WIN) + epsilon)
        scale_a = 2 * WIN * root_a
        want = peak_ref[p] + MAXLAG
        best = None
        prv = jnp.zeros_like(xr)
        cen = jnp.zeros_like(xr)
        nxt = jnp.zeros_like(xr)
        for j in range(2 * MAXLAG + 1):
            sh = (LANES - j) % LANES
            yrj = pltpu.roll(yr, sh, 1) if sh else yr
            yij = pltpu.roll(yi, sh, 1) if sh else yi
            rbj = pltpu.roll(root_full, sh, 1) if sh else root_full
            cross = _wsum(xr * yrj + xi * yij)
            ncc = cross / (scale_a * rbj)
            best = ncc if best is None else jnp.maximum(best, ncc)
            prv = jnp.where(want == j + 1, ncc, prv)
            cen = jnp.where(want == j, ncc, cen)
            nxt = jnp.where(want == j - 1, ncc, nxt)
        q_ref[p] = best
        curvature = jnp.maximum(2.0 * cen - prv - nxt, 0.25)
        d_ref[p] = peak_ref[p].astype(jnp.float32) + (nxt - prv) / (2.0 * curvature)
        return carry

    lax.fori_loop(0, fp_ref.shape[0], pair, 0)


def correlate(frame_pairs, v, peak):
    pairs = frame_pairs.shape[0]
    lines = v.shape[2]
    out = jax.ShapeDtypeStruct((pairs, lines, LANES), jnp.float32)
    vmem = pltpu.MemorySpace.VMEM
    smem = pltpu.MemorySpace.SMEM
    return pl.pallas_call(
        corr_kernel,
        out_shape=(out, out),
        in_specs=[pl.BlockSpec(memory_space=smem), pl.BlockSpec(memory_space=vmem), pl.BlockSpec(memory_space=vmem)],
        out_specs=(pl.BlockSpec(memory_space=vmem), pl.BlockSpec(memory_space=vmem)),
    )(frame_pairs, v, peak)


def from_left(block, axis):
    count = lax.axis_size(axis)
    return lax.ppermute(block, axis, [(i, i + 1) for i in range(count - 1)])


def from_right(block, axis):
    count = lax.axis_size(axis)
    return lax.ppermute(block, axis, [(i + 1, i) for i in range(count - 1)])


def beamform(extended, weights):
    return lax.conv_general_dilated(
        extended,
        weights,
        window_strides=(1,),
        padding="VALID",
        dimension_numbers=("NWC", "WIO", "NCW"),
        preferred_element_type=jnp.float32,
    )


def shards(channel_data, delay_weights, peak_lags, frame_pairs):
    frames, sample_rows, _ = channel_data.shape
    tap_count = delay_weights.shape[1]
    nx, ny, nc = (lax.axis_size(a) for a in CHAN)
    tile = lax.axis_index("tile")
    tiles = lax.axis_size("tile")

    lag_f = peak_lags.astype(jnp.float32)
    lag_prev = from_left(lag_f[:, :, -1:], "tile")
    lag_next = from_right(lag_f[:, :, :1], "tile")

    rim_rows = from_right(channel_data[:, : tap_count - 1, :], "tile")
    extended = jnp.concatenate([channel_data, rim_rows], axis=1)

    weights = delay_weights[0]
    taps, cin, cols = weights.shape
    per_dev = cols // (nx * ny * nc)
    w6 = weights.reshape(taps, cin, nx, ny, nc, per_dev)
    core = lax.axis_index("cc")
    w_mine = lax.dynamic_index_in_dim(w6, core, 4, keepdims=False).reshape(taps, cin, -1)
    w_other = lax.dynamic_index_in_dim(w6, 1 - core, 4, keepdims=False).reshape(taps, cin, -1)
    vol_other = beamform(extended, w_other)
    vol_mine = beamform(extended, w_mine)
    vol = vol_mine + lax.ppermute(vol_other, "cc", [(0, 1), (1, 0)])
    vol = vol.reshape(frames, nx * ny, per_dev, sample_rows)
    vol = lax.all_to_all(vol, ("cx", "cy"), 1, 1, tiled=True).sum(axis=1)

    head = vol[..., :HALO]
    tail = vol[..., sample_rows - HALO :]
    padded = jnp.concatenate([from_left(tail, "tile"), vol, from_right(head, "tile")], axis=2)

    line_count = per_dev // 2
    span = padded.shape[2]
    padded = jnp.pad(padded, ((0, 0), (0, 0), (0, LANES - span)))
    v = padded.reshape(frames, line_count, 2, LANES).transpose(0, 2, 1, 3)
    own = jnp.repeat(lag_f, BLK, axis=2)
    peak_full = jnp.concatenate(
        [jnp.repeat(lag_prev, 2, axis=2), own, jnp.repeat(lag_next, 2, axis=2)], axis=2
    ).astype(jnp.int32)
    peak_full = jnp.pad(peak_full, ((0, 0), (0, 0), (0, LANES - peak_full.shape[2])))
    best, displacement = correlate(frame_pairs, v, peak_full)
    quality = best[..., 2 : 2 + sample_rows]
    displacement = displacement[..., : sample_rows + 4]
    zo = lax.broadcasted_iota(jnp.int32, displacement.shape, 2)
    outside = ((tile == 0) & (zo < 2)) | ((tile == tiles - 1) & (zo >= sample_rows + 2))
    dz = jnp.where(outside, 0.0, displacement)
    strain = (
        dz[..., 0:sample_rows]
        - 8.0 * dz[..., 1 : sample_rows + 1]
        + 8.0 * dz[..., 3 : sample_rows + 3]
        - dz[..., 4 : sample_rows + 4]
    ) / 12.0
    return (quality, strain)


def solution(mesh):
    chan = mesh.shape["chan"]
    tile = mesh.shape["tile"]
    devices = mesh.devices.reshape(chan // 4, 2, 2, tile)
    fine = Mesh(devices, CHAN + ("tile",))
    return jax.shard_map(
        shards,
        mesh=fine,
        in_specs=(
            P(None, "tile", CHAN),
            P("tile", None, CHAN, None),
            P(None, CHAN, "tile"),
            P(),
        ),
        out_specs=(P(None, CHAN, "tile"), P(None, CHAN, "tile")),
        check_vma=False,
    )
```

```python
import jax
import jax.numpy as jnp
from jax import lax
from jax.sharding import Mesh, PartitionSpec as P

MAXLAG = 16
WIN = 32
BLK = 8
HALO = MAXLAG + WIN // 2 + 2

epsilon = 1e-05

CHAN = ("cx", "cy", "cc")


def window_sum(values):
    width = 1
    while width < WIN:
        n = values.shape[-1] - width
        values = values[..., :n] + values[..., width : width + n]
        width *= 2
    return values


def from_left(block, axis):
    count = lax.axis_size(axis)
    return lax.ppermute(block, axis, [(i, i + 1) for i in range(count - 1)])


def from_right(block, axis):
    count = lax.axis_size(axis)
    return lax.ppermute(block, axis, [(i + 1, i) for i in range(count - 1)])


def beamform(extended, weights):
    return lax.conv_general_dilated(
        extended,
        weights,
        window_strides=(1,),
        padding="VALID",
        dimension_numbers=("NWC", "WIO", "NCW"),
        preferred_element_type=jnp.float32,
    )


def shards(channel_data, delay_weights, peak_lags, frame_pairs):
    frames, sample_rows, _ = channel_data.shape
    tap_count = delay_weights.shape[1]
    nx, ny, nc = (lax.axis_size(a) for a in CHAN)
    tile = lax.axis_index("tile")
    tiles = lax.axis_size("tile")

    lag_f = peak_lags.astype(jnp.float32)
    lag_prev = from_left(lag_f[:, :, -1:], "tile")
    lag_next = from_right(lag_f[:, :, :1], "tile")

    weights = delay_weights[0]
    taps, cin, cols = weights.shape
    per_dev = cols // (nx * ny * nc)
    w6 = weights.reshape(taps, cin, nx, ny, nc, per_dev)
    core = lax.axis_index("cc")
    w_mine = lax.dynamic_index_in_dim(w6, core, 4, keepdims=False).reshape(taps, cin, -1)
    w_other = lax.dynamic_index_in_dim(w6, 1 - core, 4, keepdims=False).reshape(taps, cin, -1)
    swap = [(0, 1), (1, 0)]
    w_partner = lax.ppermute(w_other, "cc", swap)
    data_partner = lax.ppermute(channel_data, "cc", swap)
    rim = channel_data[:, : tap_count - 1, :]
    rim_rows = from_right(rim, "tile")
    diag = [
        (c * tiles + t + 1, (1 - c) * tiles + t) for c in range(nc) for t in range(tiles - 1)
    ]
    rim_partner = lax.ppermute(rim, ("cc", "tile"), diag)
    extended = jnp.concatenate(
        [
            jnp.concatenate([channel_data, rim_rows], axis=1),
            jnp.concatenate([data_partner, rim_partner], axis=1),
        ],
        axis=2,
    )
    vol = beamform(extended, jnp.concatenate([w_mine, w_partner], axis=1))
    vol = vol.reshape(frames, nx * ny, per_dev, sample_rows)
    edges = jnp.concatenate([vol[..., :HALO], vol[..., sample_rows - HALO :]], axis=3)
    edges = lax.all_to_all(edges, ("cx", "cy"), 1, 1, tiled=True).sum(axis=1)
    inner = vol[..., HALO : sample_rows - HALO]
    edges, inner = lax.optimization_barrier((edges, inner))
    head = edges[..., :HALO]
    tail = edges[..., HALO:]
    left = from_left(tail, "tile")
    right = from_right(head, "tile")
    inner = lax.all_to_all(inner, ("cx", "cy"), 1, 1, tiled=True).sum(axis=1)
    padded = jnp.concatenate([left, head, inner, tail, right], axis=2)

    line_count = per_dev // 2
    pair_count = frame_pairs.shape[0]
    front = padded[frame_pairs[:, 0]].reshape(pair_count, line_count, 2, -1)
    later = padded[frame_pairs[:, 1]].reshape(pair_count, line_count, 2, -1)
    out_len = sample_rows + 4
    prod_len = out_len + WIN - 1
    xr = front[:, :, 0, WIN // 2 : WIN // 2 + prod_len]
    xi = front[:, :, 1, WIN // 2 : WIN // 2 + prod_len]
    yr = later[:, :, 0]
    yi = later[:, :, 1]
    nlag = 2 * MAXLAG + 1
    prods = jnp.stack(
        [xr * yr[..., j : j + prod_len] + xi * yi[..., j : j + prod_len] for j in range(nlag)]
    )
    cross_sum = window_sum(prods)
    power_a = window_sum(xr * xr + xi * xi) / (2 * WIN)
    ey = yr * yr + yi * yi
    power_full = window_sum(ey[..., : out_len + nlag - 1 + WIN - 1]) / (2 * WIN)
    root_b = jnp.sqrt(power_full + epsilon)
    root_b = jnp.stack([root_b[..., j : j + out_len] for j in range(nlag)])
    scores = cross_sum / (2 * WIN * jnp.sqrt(power_a + epsilon)[None] * root_b)
    quality = jnp.max(scores[..., 2 : 2 + sample_rows], axis=0)

    own = jnp.repeat(lag_f, BLK, axis=2)
    peak_full = jnp.concatenate(
        [jnp.repeat(lag_prev, 2, axis=2), own, jnp.repeat(lag_next, 2, axis=2)], axis=2
    ).astype(jnp.int32)
    lag_values = jnp.arange(-MAXLAG, MAXLAG + 1, dtype=jnp.int32)[:, None, None, None]

    def pick_lag(delta):
        return jnp.sum(
            jnp.where(lag_values == peak_full[None] + delta, scores, jnp.zeros_like(scores)), axis=0
        )

    at_prev = pick_lag(-1)
    centre = pick_lag(0)
    at_next = pick_lag(1)
    curvature = jnp.maximum(2.0 * centre - at_prev - at_next, 0.25)
    displacement = peak_full.astype(jnp.float32) + (at_next - at_prev) / (2.0 * curvature)
    zo = lax.broadcasted_iota(jnp.int32, displacement.shape, 2)
    outside = ((tile == 0) & (zo < 2)) | ((tile == tiles - 1) & (zo >= sample_rows + 2))
    dz = jnp.where(outside, 0.0, displacement)
    strain = (
        dz[..., 0:sample_rows]
        - 8.0 * dz[..., 1 : sample_rows + 1]
        + 8.0 * dz[..., 3 : sample_rows + 3]
        - dz[..., 4 : sample_rows + 4]
    ) / 12.0
    return (quality, strain)


def solution(mesh):
    chan = mesh.shape["chan"]
    tile = mesh.shape["tile"]
    devices = mesh.devices.reshape(chan // 4, 2, 2, tile)
    fine = Mesh(devices, CHAN + ("tile",))
    return jax.shard_map(
        shards,
        mesh=fine,
        in_specs=(
            P(None, "tile", CHAN),
            P("tile", None, CHAN, None),
            P(None, CHAN, "tile"),
            P(),
        ),
        out_specs=(P(None, CHAN, "tile"), P(None, CHAN, "tile")),
        check_vma=False,
    )
```

```python
import jax
import jax.numpy as jnp
from jax import lax
from jax.sharding import Mesh, PartitionSpec as P

MAXLAG = 16
WIN = 32
BLK = 8
HALO = MAXLAG + WIN // 2 + 2

epsilon = 1e-05

CHAN = ("cx", "cy", "cc")


def window_sum(values):
    width = 1
    while width < WIN:
        n = values.shape[-1] - width
        values = values[..., :n] + values[..., width : width + n]
        width *= 2
    return values


def from_left(block, axis):
    count = lax.axis_size(axis)
    return lax.ppermute(block, axis, [(i, i + 1) for i in range(count - 1)])


def from_right(block, axis):
    count = lax.axis_size(axis)
    return lax.ppermute(block, axis, [(i + 1, i) for i in range(count - 1)])


def beamform(extended, weights):
    return lax.conv_general_dilated(
        extended,
        weights,
        window_strides=(1,),
        padding="VALID",
        dimension_numbers=("NWC", "WIO", "NCW"),
        preferred_element_type=jnp.float32,
    )


def shards(channel_data, delay_weights, peak_lags, frame_pairs):
    frames, sample_rows, _ = channel_data.shape
    tap_count = delay_weights.shape[1]
    nx, ny, nc = (lax.axis_size(a) for a in CHAN)
    tile = lax.axis_index("tile")
    tiles = lax.axis_size("tile")

    lag_f = peak_lags.astype(jnp.float32)
    lag_prev = from_left(lag_f[:, :, -1:], "tile")
    lag_next = from_right(lag_f[:, :, :1], "tile")

    rim_rows = from_right(channel_data[:, : tap_count - 1, :], "tile")
    main_rows = sample_rows - tap_count + 1
    tail_rows = jnp.concatenate([channel_data[:, main_rows:, :], rim_rows], axis=1)

    weights = delay_weights[0]
    taps, cin, cols = weights.shape
    per_dev = cols // (nx * ny * nc)
    w6 = weights.reshape(taps, cin, nx, ny, nc, per_dev)
    core = lax.axis_index("cc")
    w_mine = lax.dynamic_index_in_dim(w6, core, 4, keepdims=False).reshape(taps, cin, -1)
    w_other = lax.dynamic_index_in_dim(w6, 1 - core, 4, keepdims=False).reshape(taps, cin, -1)

    def beam(w):
        return jnp.concatenate([beamform(channel_data, w), beamform(tail_rows, w)], axis=2)

    vol_other = beam(w_other)
    vol_mine = beam(w_mine)
    swap = [(0, 1), (1, 0)]
    to_next = [(c * tiles + t, (1 - c) * tiles + t + 1) for c in range(nc) for t in range(tiles - 1)]
    to_prev = [(c * tiles + t + 1, (1 - c) * tiles + t) for c in range(nc) for t in range(tiles - 1)]
    left = from_left(vol_mine[..., sample_rows - HALO :], "tile") + lax.ppermute(
        vol_other[..., sample_rows - HALO :], ("cc", "tile"), to_next
    )
    right = from_right(vol_mine[..., :HALO], "tile") + lax.ppermute(
        vol_other[..., :HALO], ("cc", "tile"), to_prev
    )
    centre = vol_mine + lax.ppermute(vol_other, "cc", swap)
    vol = jnp.concatenate([left, centre, right], axis=2)
    span = vol.shape[2]
    vol = vol.reshape(frames, nx * ny, per_dev, span)
    padded = lax.all_to_all(vol, ("cx", "cy"), 1, 1, tiled=True).sum(axis=1)

    line_count = per_dev // 2
    pair_count = frame_pairs.shape[0]
    front = padded[frame_pairs[:, 0]].reshape(pair_count, line_count, 2, -1)
    later = padded[frame_pairs[:, 1]].reshape(pair_count, line_count, 2, -1)
    out_len = sample_rows + 4
    prod_len = out_len + WIN - 1
    xr = front[:, :, 0, WIN // 2 : WIN // 2 + prod_len]
    xi = front[:, :, 1, WIN // 2 : WIN // 2 + prod_len]
    yr = later[:, :, 0]
    yi = later[:, :, 1]
    nlag = 2 * MAXLAG + 1
    prods = jnp.stack(
        [xr * yr[..., j : j + prod_len] + xi * yi[..., j : j + prod_len] for j in range(nlag)]
    )
    cross_sum = window_sum(prods)
    power_a = window_sum(xr * xr + xi * xi) / (2 * WIN)
    ey = yr * yr + yi * yi
    power_full = window_sum(ey[..., : out_len + nlag - 1 + WIN - 1]) / (2 * WIN)
    root_b = jnp.sqrt(power_full + epsilon)
    root_b = jnp.stack([root_b[..., j : j + out_len] for j in range(nlag)])
    scores = cross_sum / (2 * WIN * jnp.sqrt(power_a + epsilon)[None] * root_b)
    quality = jnp.max(scores[..., 2 : 2 + sample_rows], axis=0)

    own = jnp.repeat(lag_f, BLK, axis=2)
    peak_full = jnp.concatenate(
        [jnp.repeat(lag_prev, 2, axis=2), own, jnp.repeat(lag_next, 2, axis=2)], axis=2
    ).astype(jnp.int32)
    lag_values = jnp.arange(-MAXLAG, MAXLAG + 1, dtype=jnp.int32)[:, None, None, None]

    def pick_lag(delta):
        return jnp.sum(
            jnp.where(lag_values == peak_full[None] + delta, scores, jnp.zeros_like(scores)), axis=0
        )

    at_prev = pick_lag(-1)
    centre = pick_lag(0)
    at_next = pick_lag(1)
    curvature = jnp.maximum(2.0 * centre - at_prev - at_next, 0.25)
    displacement = peak_full.astype(jnp.float32) + (at_next - at_prev) / (2.0 * curvature)
    zo = lax.broadcasted_iota(jnp.int32, displacement.shape, 2)
    outside = ((tile == 0) & (zo < 2)) | ((tile == tiles - 1) & (zo >= sample_rows + 2))
    dz = jnp.where(outside, 0.0, displacement)
    strain = (
        dz[..., 0:sample_rows]
        - 8.0 * dz[..., 1 : sample_rows + 1]
        + 8.0 * dz[..., 3 : sample_rows + 3]
        - dz[..., 4 : sample_rows + 4]
    ) / 12.0
    return (quality, strain)


def solution(mesh):
    chan = mesh.shape["chan"]
    tile = mesh.shape["tile"]
    devices = mesh.devices.reshape(chan // 4, 2, 2, tile)
    fine = Mesh(devices, CHAN + ("tile",))
    return jax.shard_map(
        shards,
        mesh=fine,
        in_specs=(
            P(None, "tile", CHAN),
            P("tile", None, CHAN, None),
            P(None, CHAN, "tile"),
            P(),
        ),
        out_specs=(P(None, CHAN, "tile"), P(None, CHAN, "tile")),
        check_vma=False,
    )
```

```python
import jax
import jax.numpy as jnp
from jax import lax
from jax.sharding import Mesh, PartitionSpec as P

MAXLAG = 16
WIN = 32
BLK = 8
HALO = MAXLAG + WIN // 2 + 2

epsilon = 1e-05

CHAN = ("cx", "cy", "cc")


def window_sum(values):
    width = 1
    while width < WIN:
        n = values.shape[-1] - width
        values = values[..., :n] + values[..., width : width + n]
        width *= 2
    return values


def from_left(block, axis):
    count = lax.axis_size(axis)
    return lax.ppermute(block, axis, [(i, i + 1) for i in range(count - 1)])


def from_right(block, axis):
    count = lax.axis_size(axis)
    return lax.ppermute(block, axis, [(i + 1, i) for i in range(count - 1)])


def beamform(extended, weights):
    return lax.conv_general_dilated(
        extended,
        weights,
        window_strides=(1,),
        padding="VALID",
        dimension_numbers=("NWC", "WIO", "NCW"),
        preferred_element_type=jnp.float32,
    )


def shards(channel_data, delay_weights, peak_lags, frame_pairs):
    frames, sample_rows, _ = channel_data.shape
    tap_count = delay_weights.shape[1]
    nx, ny, nc = (lax.axis_size(a) for a in CHAN)
    tile = lax.axis_index("tile")
    tiles = lax.axis_size("tile")

    lag_f = peak_lags.astype(jnp.float32)
    pairs_n, lines_n, _ = peak_lags.shape
    rim = channel_data[:, : tap_count - 1, :]
    sent = jnp.concatenate(
        [rim.reshape(-1), peak_lags[:, :, 0].astype(channel_data.dtype).reshape(-1)]
    )
    got = from_right(sent, "tile")
    rim_rows = got[: rim.size].reshape(rim.shape)
    lag_next = got[rim.size :].astype(jnp.float32).reshape(pairs_n, lines_n, 1)
    main_rows = sample_rows - tap_count + 1
    tail_rows = jnp.concatenate([channel_data[:, main_rows:, :], rim_rows], axis=1)

    weights = delay_weights[0]
    taps, cin, cols = weights.shape
    per_dev = cols // (nx * ny * nc)
    w6 = weights.reshape(taps, cin, nx, ny, nc, per_dev)
    core = lax.axis_index("cc")
    w_mine = lax.dynamic_index_in_dim(w6, core, 4, keepdims=False).reshape(taps, cin, -1)
    w_other = lax.dynamic_index_in_dim(w6, 1 - core, 4, keepdims=False).reshape(taps, cin, -1)
    def beam(w):
        return jnp.concatenate([beamform(channel_data, w), beamform(tail_rows, w)], axis=2)

    vol_other = beam(w_other)
    vol_mine = beam(w_mine)
    vol = vol_mine + lax.ppermute(vol_other, "cc", [(0, 1), (1, 0)])
    vol = vol.reshape(frames, nx * ny, per_dev, sample_rows)
    vol = lax.all_to_all(vol, ("cx", "cy"), 1, 1, tiled=True).sum(axis=1)

    head = vol[..., :HALO]
    tail = vol[..., sample_rows - HALO :]
    sent = jnp.concatenate([tail.reshape(-1), lag_f[:, :, -1].reshape(-1)])
    got = from_left(sent, "tile")
    left = got[: tail.size].reshape(tail.shape)
    lag_prev = got[tail.size :].reshape(pairs_n, lines_n, 1)
    padded = jnp.concatenate([left, vol, from_right(head, "tile")], axis=2)

    line_count = per_dev // 2
    pair_count = frame_pairs.shape[0]
    front = padded[frame_pairs[:, 0]].reshape(pair_count, line_count, 2, -1)
    later = padded[frame_pairs[:, 1]].reshape(pair_count, line_count, 2, -1)
    out_len = sample_rows + 4
    prod_len = out_len + WIN - 1
    xr = front[:, :, 0, WIN // 2 : WIN // 2 + prod_len]
    xi = front[:, :, 1, WIN // 2 : WIN // 2 + prod_len]
    yr = later[:, :, 0]
    yi = later[:, :, 1]
    nlag = 2 * MAXLAG + 1
    prods = jnp.stack(
        [xr * yr[..., j : j + prod_len] + xi * yi[..., j : j + prod_len] for j in range(nlag)]
    )
    cross_sum = window_sum(prods)
    power_a = window_sum(xr * xr + xi * xi) / (2 * WIN)
    ey = yr * yr + yi * yi
    power_full = window_sum(ey[..., : out_len + nlag - 1 + WIN - 1]) / (2 * WIN)
    root_b = jnp.sqrt(power_full + epsilon)
    root_b = jnp.stack([root_b[..., j : j + out_len] for j in range(nlag)])
    scores = cross_sum / (2 * WIN * jnp.sqrt(power_a + epsilon)[None] * root_b)
    quality = jnp.max(scores[..., 2 : 2 + sample_rows], axis=0)

    own = jnp.repeat(lag_f, BLK, axis=2)
    peak_full = jnp.concatenate(
        [jnp.repeat(lag_prev, 2, axis=2), own, jnp.repeat(lag_next, 2, axis=2)], axis=2
    ).astype(jnp.int32)
    lag_values = jnp.arange(-MAXLAG, MAXLAG + 1, dtype=jnp.int32)[:, None, None, None]

    def pick_lag(delta):
        return jnp.sum(
            jnp.where(lag_values == peak_full[None] + delta, scores, jnp.zeros_like(scores)), axis=0
        )

    at_prev = pick_lag(-1)
    centre = pick_lag(0)
    at_next = pick_lag(1)
    curvature = jnp.maximum(2.0 * centre - at_prev - at_next, 0.25)
    displacement = peak_full.astype(jnp.float32) + (at_next - at_prev) / (2.0 * curvature)
    zo = lax.broadcasted_iota(jnp.int32, displacement.shape, 2)
    outside = ((tile == 0) & (zo < 2)) | ((tile == tiles - 1) & (zo >= sample_rows + 2))
    dz = jnp.where(outside, 0.0, displacement)
    strain = (
        dz[..., 0:sample_rows]
        - 8.0 * dz[..., 1 : sample_rows + 1]
        + 8.0 * dz[..., 3 : sample_rows + 3]
        - dz[..., 4 : sample_rows + 4]
    ) / 12.0
    return (quality, strain)


def solution(mesh):
    chan = mesh.shape["chan"]
    tile = mesh.shape["tile"]
    devices = mesh.devices.reshape(chan // 4, 2, 2, tile)
    fine = Mesh(devices, CHAN + ("tile",))
    return jax.shard_map(
        shards,
        mesh=fine,
        in_specs=(
            P(None, "tile", CHAN),
            P("tile", None, CHAN, None),
            P(None, CHAN, "tile"),
            P(),
        ),
        out_specs=(P(None, CHAN, "tile"), P(None, CHAN, "tile")),
        check_vma=False,
    )
```

```python
import jax
import jax.numpy as jnp
from jax import lax
from jax.sharding import Mesh, PartitionSpec as P

MAXLAG = 16
WIN = 32
BLK = 8
HALO = MAXLAG + WIN // 2 + 2

epsilon = 1e-05

CHAN = ("cx", "cy", "cc")


def window_sum(values):
    width = 1
    while width < WIN:
        n = values.shape[-1] - width
        values = values[..., :n] + values[..., width : width + n]
        width *= 2
    return values


def from_left(block, axis):
    count = lax.axis_size(axis)
    return lax.ppermute(block, axis, [(i, i + 1) for i in range(count - 1)])


def from_right(block, axis):
    count = lax.axis_size(axis)
    return lax.ppermute(block, axis, [(i + 1, i) for i in range(count - 1)])


def beamform(extended, weights):
    return lax.conv_general_dilated(
        extended,
        weights,
        window_strides=(1,),
        padding="VALID",
        dimension_numbers=("NWC", "WIO", "NCW"),
        preferred_element_type=jnp.float32,
    )


def shards(channel_data, delay_weights, peak_lags, frame_pairs):
    frames, sample_rows, _ = channel_data.shape
    tap_count = delay_weights.shape[1]
    nx, ny, nc = (lax.axis_size(a) for a in CHAN)
    tile = lax.axis_index("tile")
    tiles = lax.axis_size("tile")

    lag_f = peak_lags.astype(jnp.float32)
    pairs_n, lines_n, _ = peak_lags.shape
    rim = channel_data[:, : tap_count - 1, :]
    sent = jnp.concatenate(
        [rim.reshape(-1), peak_lags[:, :, 0].astype(channel_data.dtype).reshape(-1)]
    )
    got = from_right(sent, "tile")
    rim_rows = got[: rim.size].reshape(rim.shape)
    lag_next = got[rim.size :].astype(jnp.float32).reshape(pairs_n, lines_n, 1)
    main_rows = sample_rows - tap_count + 1
    tail_rows = jnp.concatenate([channel_data[:, main_rows:, :], rim_rows], axis=1)

    weights = delay_weights[0]
    taps, cin, cols = weights.shape
    per_dev = cols // (nx * ny * nc)
    w6 = weights.reshape(taps, cin, nx, ny, nc, per_dev)
    core = lax.axis_index("cc")
    w_mine = lax.dynamic_index_in_dim(w6, core, 4, keepdims=False).reshape(taps, cin, -1)
    w_other = lax.dynamic_index_in_dim(w6, 1 - core, 4, keepdims=False).reshape(taps, cin, -1)
    def beam(w):
        return jnp.concatenate([beamform(channel_data, w), beamform(tail_rows, w)], axis=2)

    vol_other = beam(w_other)
    vol_mine = beam(w_mine)
    vol = vol_mine + lax.ppermute(vol_other, "cc", [(0, 1), (1, 0)])
    vol = vol.reshape(frames, nx * ny, per_dev, sample_rows)
    vol = lax.all_to_all(vol, ("cx", "cy"), 1, 1, tiled=True).sum(axis=1)

    head = vol[..., :HALO]
    tail = vol[..., sample_rows - HALO :]
    sent = jnp.concatenate([tail.reshape(-1), lag_f[:, :, -1].reshape(-1)])
    got = from_left(sent, "tile")
    left = got[: tail.size].reshape(tail.shape)
    lag_prev = got[tail.size :].reshape(pairs_n, lines_n, 1)
    padded = jnp.concatenate([left, vol, from_right(head, "tile")], axis=2)

    line_count = per_dev // 2
    pair_count = frame_pairs.shape[0]
    front = padded[frame_pairs[:, 0]].reshape(pair_count, line_count, 2, -1)
    later = padded[frame_pairs[:, 1]].reshape(pair_count, line_count, 2, -1)
    out_len = sample_rows + 4
    prod_len = out_len + WIN - 1
    xr = front[:, :, 0, WIN // 2 : WIN // 2 + prod_len]
    xi = front[:, :, 1, WIN // 2 : WIN // 2 + prod_len]
    yr = later[:, :, 0]
    yi = later[:, :, 1]
    nlag = 2 * MAXLAG + 1
    prods = jnp.stack(
        [xr * yr[..., j : j + prod_len] + xi * yi[..., j : j + prod_len] for j in range(nlag)]
    )
    cross_sum = window_sum(prods)
    power_a = window_sum(xr * xr + xi * xi) / (2 * WIN)
    ey = yr * yr + yi * yi
    power_full = window_sum(ey[..., : out_len + nlag - 1 + WIN - 1]) / (2 * WIN)
    root_b = jnp.sqrt(power_full + epsilon)
    root_a = 2 * WIN * jnp.sqrt(power_a + epsilon)

    own = jnp.repeat(lag_f, BLK, axis=2)
    peak_full = jnp.concatenate(
        [jnp.repeat(lag_prev, 2, axis=2), own, jnp.repeat(lag_next, 2, axis=2)], axis=2
    ).astype(jnp.int32)
    want = peak_full + MAXLAG
    best = None
    at_prev = jnp.zeros_like(root_a)
    centre = jnp.zeros_like(root_a)
    at_next = jnp.zeros_like(root_a)
    for j in range(nlag):
        score = cross_sum[j] / (root_a * root_b[..., j : j + out_len])
        best = score if best is None else jnp.maximum(best, score)
        at_prev = jnp.where(want == j + 1, score, at_prev)
        centre = jnp.where(want == j, score, centre)
        at_next = jnp.where(want == j - 1, score, at_next)
    quality = best[..., 2 : 2 + sample_rows]

    curvature = jnp.maximum(2.0 * centre - at_prev - at_next, 0.25)
    displacement = peak_full.astype(jnp.float32) + (at_next - at_prev) / (2.0 * curvature)
    zo = lax.broadcasted_iota(jnp.int32, displacement.shape, 2)
    outside = ((tile == 0) & (zo < 2)) | ((tile == tiles - 1) & (zo >= sample_rows + 2))
    dz = jnp.where(outside, 0.0, displacement)
    strain = (
        dz[..., 0:sample_rows]
        - 8.0 * dz[..., 1 : sample_rows + 1]
        + 8.0 * dz[..., 3 : sample_rows + 3]
        - dz[..., 4 : sample_rows + 4]
    ) / 12.0
    return (quality, strain)


def solution(mesh):
    chan = mesh.shape["chan"]
    tile = mesh.shape["tile"]
    devices = mesh.devices.reshape(chan // 4, 2, 2, tile)
    fine = Mesh(devices, CHAN + ("tile",))
    return jax.shard_map(
        shards,
        mesh=fine,
        in_specs=(
            P(None, "tile", CHAN),
            P("tile", None, CHAN, None),
            P(None, CHAN, "tile"),
            P(),
        ),
        out_specs=(P(None, CHAN, "tile"), P(None, CHAN, "tile")),
        check_vma=False,
    )
```

```python
import jax
import jax.numpy as jnp
from jax import lax
from jax.sharding import Mesh, PartitionSpec as P

MAXLAG = 16
WIN = 32
BLK = 8
HALO = MAXLAG + WIN // 2 + 2

epsilon = 1e-05

CHAN = ("cx", "cy", "cc")


def window_sum(values):
    width = 1
    while width < WIN:
        n = values.shape[-1] - width
        values = values[..., :n] + values[..., width : width + n]
        width *= 2
    return values


def from_left(block, axis):
    count = lax.axis_size(axis)
    return lax.ppermute(block, axis, [(i, i + 1) for i in range(count - 1)])


def from_right(block, axis):
    count = lax.axis_size(axis)
    return lax.ppermute(block, axis, [(i + 1, i) for i in range(count - 1)])


def beamform(extended, weights):
    return lax.conv_general_dilated(
        extended,
        weights,
        window_strides=(1,),
        padding="VALID",
        dimension_numbers=("NWC", "WIO", "CNW"),
        preferred_element_type=jnp.float32,
    )


def shards(channel_data, delay_weights, peak_lags, frame_pairs):
    frames, sample_rows, _ = channel_data.shape
    tap_count = delay_weights.shape[1]
    nx, ny, nc = (lax.axis_size(a) for a in CHAN)
    tile = lax.axis_index("tile")
    tiles = lax.axis_size("tile")

    lag_f = peak_lags.astype(jnp.float32)
    pairs_n, lines_n, _ = peak_lags.shape
    rim = channel_data[:, : tap_count - 1, :]
    sent = jnp.concatenate(
        [rim.reshape(-1), peak_lags[:, :, 0].astype(channel_data.dtype).reshape(-1)]
    )
    got = from_right(sent, "tile")
    rim_rows = got[: rim.size].reshape(rim.shape)
    lag_next = got[rim.size :].astype(jnp.float32).reshape(pairs_n, lines_n, 1)
    main_rows = sample_rows - tap_count + 1
    tail_rows = jnp.concatenate([channel_data[:, main_rows:, :], rim_rows], axis=1)

    weights = delay_weights[0]
    taps, cin, cols = weights.shape
    per_dev = cols // (nx * ny * nc)
    w6 = weights.reshape(taps, cin, nx, ny, nc, per_dev)
    core = lax.axis_index("cc")
    w_mine = lax.dynamic_index_in_dim(w6, core, 4, keepdims=False).reshape(taps, cin, -1)
    w_other = lax.dynamic_index_in_dim(w6, 1 - core, 4, keepdims=False).reshape(taps, cin, -1)
    def beam(w):
        return jnp.concatenate([beamform(channel_data, w), beamform(tail_rows, w)], axis=2)

    vol_other = beam(w_other)
    vol_mine = beam(w_mine)
    vol = vol_mine + lax.ppermute(vol_other, "cc", [(0, 1), (1, 0)])
    vol = vol.reshape(nx * ny, per_dev, frames, sample_rows)
    vol = lax.all_to_all(vol, ("cx", "cy"), 0, 0, tiled=True).sum(axis=0).transpose(1, 0, 2)

    head = vol[..., :HALO]
    tail = vol[..., sample_rows - HALO :]
    sent = jnp.concatenate([tail.reshape(-1), lag_f[:, :, -1].reshape(-1)])
    got = from_left(sent, "tile")
    left = got[: tail.size].reshape(tail.shape)
    lag_prev = got[tail.size :].reshape(pairs_n, lines_n, 1)
    padded = jnp.concatenate([left, vol, from_right(head, "tile")], axis=2)

    line_count = per_dev // 2
    pair_count = frame_pairs.shape[0]
    front = padded[frame_pairs[:, 0]].reshape(pair_count, line_count, 2, -1)
    later = padded[frame_pairs[:, 1]].reshape(pair_count, line_count, 2, -1)
    out_len = sample_rows + 4
    prod_len = out_len + WIN - 1
    xr = front[:, :, 0, WIN // 2 : WIN // 2 + prod_len]
    xi = front[:, :, 1, WIN // 2 : WIN // 2 + prod_len]
    yr = later[:, :, 0]
    yi = later[:, :, 1]
    nlag = 2 * MAXLAG + 1
    prods = jnp.stack(
        [xr * yr[..., j : j + prod_len] + xi * yi[..., j : j + prod_len] for j in range(nlag)]
    )
    cross_sum = window_sum(prods)
    power_a = window_sum(xr * xr + xi * xi) / (2 * WIN)
    ey = yr * yr + yi * yi
    power_full = window_sum(ey[..., : out_len + nlag - 1 + WIN - 1]) / (2 * WIN)
    root_b = jnp.sqrt(power_full + epsilon)
    root_a = 2 * WIN * jnp.sqrt(power_a + epsilon)

    own = jnp.repeat(lag_f, BLK, axis=2)
    peak_full = jnp.concatenate(
        [jnp.repeat(lag_prev, 2, axis=2), own, jnp.repeat(lag_next, 2, axis=2)], axis=2
    ).astype(jnp.int32)
    want = peak_full + MAXLAG
    best = None
    at_prev = jnp.zeros_like(root_a)
    centre = jnp.zeros_like(root_a)
    at_next = jnp.zeros_like(root_a)
    for j in range(nlag):
        score = cross_sum[j] / (root_a * root_b[..., j : j + out_len])
        best = score if best is None else jnp.maximum(best, score)
        at_prev = jnp.where(want == j + 1, score, at_prev)
        centre = jnp.where(want == j, score, centre)
        at_next = jnp.where(want == j - 1, score, at_next)
    quality = best[..., 2 : 2 + sample_rows]

    curvature = jnp.maximum(2.0 * centre - at_prev - at_next, 0.25)
    displacement = peak_full.astype(jnp.float32) + (at_next - at_prev) / (2.0 * curvature)
    zo = lax.broadcasted_iota(jnp.int32, displacement.shape, 2)
    outside = ((tile == 0) & (zo < 2)) | ((tile == tiles - 1) & (zo >= sample_rows + 2))
    dz = jnp.where(outside, 0.0, displacement)
    strain = (
        dz[..., 0:sample_rows]
        - 8.0 * dz[..., 1 : sample_rows + 1]
        + 8.0 * dz[..., 3 : sample_rows + 3]
        - dz[..., 4 : sample_rows + 4]
    ) / 12.0
    return (quality, strain)


def solution(mesh):
    chan = mesh.shape["chan"]
    tile = mesh.shape["tile"]
    devices = mesh.devices.reshape(chan // 4, 2, 2, tile)
    fine = Mesh(devices, CHAN + ("tile",))
    return jax.shard_map(
        shards,
        mesh=fine,
        in_specs=(
            P(None, "tile", CHAN),
            P("tile", None, CHAN, None),
            P(None, CHAN, "tile"),
            P(),
        ),
        out_specs=(P(None, CHAN, "tile"), P(None, CHAN, "tile")),
        check_vma=False,
    )
```

```python
import jax
import jax.numpy as jnp
from jax import lax
from jax.sharding import Mesh, PartitionSpec as P

MAXLAG = 16
WIN = 32
BLK = 8
HALO = MAXLAG + WIN // 2 + 2

epsilon = 1e-05

CHAN = ("cx", "cy", "cc")


def window_sum(values):
    width = 1
    while width < WIN:
        n = values.shape[-1] - width
        values = values[..., :n] + values[..., width : width + n]
        width *= 2
    return values


def lag_scores(vol, frame_pairs, line_count, peak):
    lead = vol.shape[:-3]
    pair_count = frame_pairs.shape[0]
    front = jnp.take(vol, frame_pairs[:, 0], axis=-3).reshape(lead + (pair_count, line_count, 2, -1))
    later = jnp.take(vol, frame_pairs[:, 1], axis=-3).reshape(lead + (pair_count, line_count, 2, -1))
    out_len = vol.shape[-1] - (2 * MAXLAG + WIN - 1)
    prod_len = out_len + WIN - 1
    xr = front[..., 0, WIN // 2 : WIN // 2 + prod_len]
    xi = front[..., 1, WIN // 2 : WIN // 2 + prod_len]
    yr = later[..., 0, :]
    yi = later[..., 1, :]
    nlag = 2 * MAXLAG + 1
    prods = jnp.stack(
        [xr * yr[..., j : j + prod_len] + xi * yi[..., j : j + prod_len] for j in range(nlag)]
    )
    cross_sum = window_sum(prods)
    power_a = window_sum(xr * xr + xi * xi) / (2 * WIN)
    ey = yr * yr + yi * yi
    power_full = window_sum(ey[..., : out_len + nlag - 1 + WIN - 1]) / (2 * WIN)
    root_b = jnp.sqrt(power_full + epsilon)
    root_a = 2 * WIN * jnp.sqrt(power_a + epsilon)
    want = peak + MAXLAG
    best = None
    at_prev = jnp.zeros_like(root_a)
    centre = jnp.zeros_like(root_a)
    at_next = jnp.zeros_like(root_a)
    for j in range(nlag):
        score = cross_sum[j] / (root_a * root_b[..., j : j + out_len])
        best = score if best is None else jnp.maximum(best, score)
        at_prev = jnp.where(want == j + 1, score, at_prev)
        centre = jnp.where(want == j, score, centre)
        at_next = jnp.where(want == j - 1, score, at_next)
    curvature = jnp.maximum(2.0 * centre - at_prev - at_next, 0.25)
    displacement = peak.astype(jnp.float32) + (at_next - at_prev) / (2.0 * curvature)
    return best, displacement


def from_left(block, axis):
    count = lax.axis_size(axis)
    return lax.ppermute(block, axis, [(i, i + 1) for i in range(count - 1)])


def from_right(block, axis):
    count = lax.axis_size(axis)
    return lax.ppermute(block, axis, [(i + 1, i) for i in range(count - 1)])


def beamform(extended, weights):
    return lax.conv_general_dilated(
        extended,
        weights,
        window_strides=(1,),
        padding="VALID",
        dimension_numbers=("NWC", "WIO", "NCW"),
        preferred_element_type=jnp.float32,
    )


def shards(channel_data, delay_weights, peak_lags, frame_pairs):
    frames, sample_rows, _ = channel_data.shape
    tap_count = delay_weights.shape[1]
    nx, ny, nc = (lax.axis_size(a) for a in CHAN)
    tile = lax.axis_index("tile")
    tiles = lax.axis_size("tile")

    lag_f = peak_lags.astype(jnp.float32)
    pairs_n, lines_n, _ = peak_lags.shape
    rim = channel_data[:, : tap_count - 1, :]
    sent = jnp.concatenate(
        [rim.reshape(-1), peak_lags[:, :, 0].astype(channel_data.dtype).reshape(-1)]
    )
    got = from_right(sent, "tile")
    rim_rows = got[: rim.size].reshape(rim.shape)
    lag_next = got[rim.size :].astype(jnp.float32).reshape(pairs_n, lines_n, 1)
    main_rows = sample_rows - tap_count + 1
    tail_rows = jnp.concatenate([channel_data[:, main_rows:, :], rim_rows], axis=1)

    weights = delay_weights[0]
    taps, cin, cols = weights.shape
    per_dev = cols // (nx * ny * nc)
    w6 = weights.reshape(taps, cin, nx, ny, nc, per_dev)
    core = lax.axis_index("cc")
    w_mine = lax.dynamic_index_in_dim(w6, core, 4, keepdims=False).reshape(taps, cin, -1)
    w_other = lax.dynamic_index_in_dim(w6, 1 - core, 4, keepdims=False).reshape(taps, cin, -1)
    def beam(w):
        return jnp.concatenate([beamform(channel_data, w), beamform(tail_rows, w)], axis=2)

    vol_other = beam(w_other)
    vol_mine = beam(w_mine)
    vol = vol_mine + lax.ppermute(vol_other, "cc", [(0, 1), (1, 0)])
    vol = vol.reshape(frames, nx * ny, per_dev, sample_rows)
    vol = lax.all_to_all(vol, ("cx", "cy"), 1, 1, tiled=True).sum(axis=1)

    head = vol[..., :HALO]
    tail = vol[..., sample_rows - HALO :]
    sent = jnp.concatenate([tail.reshape(-1), lag_f[:, :, -1].reshape(-1)])
    got = from_left(sent, "tile")
    left = got[: tail.size].reshape(tail.shape)
    lag_prev = got[tail.size :].reshape(pairs_n, lines_n, 1)
    right = from_right(head, "tile")

    own = jnp.repeat(lag_f, BLK, axis=2)
    peak_full = jnp.concatenate(
        [jnp.repeat(lag_prev, 2, axis=2), own, jnp.repeat(lag_next, 2, axis=2)], axis=2
    ).astype(jnp.int32)
    line_count = per_dev // 2
    reach = 2 * MAXLAG + WIN - 1
    out_len = sample_rows + 4
    inner_lo = HALO
    inner_len = sample_rows - 2 * HALO + 4
    inner = lag_scores(
        vol[..., : inner_len + reach],
        frame_pairs,
        line_count,
        peak_full[..., inner_lo : inner_lo + inner_len],
    )
    edge_len = (out_len - inner_len) // 2
    edge_rows = edge_len + reach
    right_from = out_len - edge_len - HALO
    edges = jnp.stack(
        [
            jnp.concatenate([left, vol[..., : edge_rows - HALO]], axis=2),
            jnp.concatenate([vol[..., right_from:], right[..., : edge_rows - (sample_rows - right_from)]], axis=2),
        ]
    )
    edge_peak = jnp.stack([peak_full[..., :edge_len], peak_full[..., out_len - edge_len :]])
    outer = lag_scores(edges, frame_pairs, line_count, edge_peak)
    best, displacement = (
        jnp.concatenate([o[0], i, o[1]], axis=-1) for i, o in zip(inner, outer)
    )
    quality = best[..., 2 : 2 + sample_rows]
    zo = lax.broadcasted_iota(jnp.int32, displacement.shape, 2)
    outside = ((tile == 0) & (zo < 2)) | ((tile == tiles - 1) & (zo >= sample_rows + 2))
    dz = jnp.where(outside, 0.0, displacement)
    strain = (
        dz[..., 0:sample_rows]
        - 8.0 * dz[..., 1 : sample_rows + 1]
        + 8.0 * dz[..., 3 : sample_rows + 3]
        - dz[..., 4 : sample_rows + 4]
    ) / 12.0
    return (quality, strain)


def solution(mesh):
    chan = mesh.shape["chan"]
    tile = mesh.shape["tile"]
    devices = mesh.devices.reshape(chan // 4, 2, 2, tile)
    fine = Mesh(devices, CHAN + ("tile",))
    return jax.shard_map(
        shards,
        mesh=fine,
        in_specs=(
            P(None, "tile", CHAN),
            P("tile", None, CHAN, None),
            P(None, CHAN, "tile"),
            P(),
        ),
        out_specs=(P(None, CHAN, "tile"), P(None, CHAN, "tile")),
        check_vma=False,
    )
```

```python
import jax
import jax.numpy as jnp
from jax import lax
from jax.sharding import Mesh, PartitionSpec as P

MAXLAG = 16
WIN = 32
BLK = 8
HALO = MAXLAG + WIN // 2 + 2

epsilon = 1e-05

CHAN = ("cx", "cy", "cc")


def window_sum(values):
    width = 1
    while width < WIN:
        n = values.shape[-1] - width
        values = values[..., :n] + values[..., width : width + n]
        width *= 2
    return values


def from_left(block, axis):
    count = lax.axis_size(axis)
    return lax.ppermute(block, axis, [(i, i + 1) for i in range(count - 1)])


def from_right(block, axis):
    count = lax.axis_size(axis)
    return lax.ppermute(block, axis, [(i + 1, i) for i in range(count - 1)])


def beamform(extended, weights):
    return lax.conv_general_dilated(
        extended,
        weights,
        window_strides=(1,),
        padding="VALID",
        dimension_numbers=("NWC", "WIO", "NCW"),
        preferred_element_type=jnp.float32,
    )


def shards(channel_data, delay_weights, peak_lags, frame_pairs):
    frames, sample_rows, _ = channel_data.shape
    tap_count = delay_weights.shape[1]
    nx, ny, nc = (lax.axis_size(a) for a in CHAN)
    tile = lax.axis_index("tile")
    tiles = lax.axis_size("tile")

    lag_f = peak_lags.astype(jnp.float32)
    pairs_n, lines_n, _ = peak_lags.shape
    rim = channel_data[:, : tap_count - 1, :]
    first_lags = peak_lags[:, :, 0].astype(channel_data.dtype).reshape(-1)
    plane = rim.shape[1] * rim.shape[2]
    first_lags = jnp.pad(first_lags, (0, plane - first_lags.size)).reshape((1,) + rim.shape[1:])
    got = from_right(jnp.concatenate([rim, first_lags], axis=0), "tile")
    rim_rows = got[:frames]
    lag_next = got[frames].reshape(-1)[: pairs_n * lines_n].astype(jnp.float32)
    lag_next = lag_next.reshape(pairs_n, lines_n, 1)
    main_rows = sample_rows - tap_count + 1
    tail_rows = jnp.concatenate([channel_data[:, main_rows:, :], rim_rows], axis=1)

    weights = delay_weights[0]
    taps, cin, cols = weights.shape
    per_dev = cols // (nx * ny * nc)
    w6 = weights.reshape(taps, cin, nx, ny, nc, per_dev)
    core = lax.axis_index("cc")
    w_mine = lax.dynamic_index_in_dim(w6, core, 4, keepdims=False).reshape(taps, cin, -1)
    w_other = lax.dynamic_index_in_dim(w6, 1 - core, 4, keepdims=False).reshape(taps, cin, -1)
    def beam(w):
        return jnp.concatenate([beamform(channel_data, w), beamform(tail_rows, w)], axis=2)

    vol_other = beam(w_other)
    vol_mine = beam(w_mine)
    vol = vol_mine + lax.ppermute(vol_other, "cc", [(0, 1), (1, 0)])
    vol = vol.reshape(frames, nx * ny, per_dev, sample_rows)
    vol = lax.all_to_all(vol, ("cx", "cy"), 1, 1, tiled=True).sum(axis=1)

    head = vol[..., :HALO]
    tail = vol[..., sample_rows - HALO :]
    sent = jnp.concatenate([tail.reshape(-1), lag_f[:, :, -1].reshape(-1)])
    got = from_left(sent, "tile")
    left = got[: tail.size].reshape(tail.shape)
    lag_prev = got[tail.size :].reshape(pairs_n, lines_n, 1)
    padded = jnp.concatenate([left, vol, from_right(head, "tile")], axis=2)

    line_count = per_dev // 2
    pair_count = frame_pairs.shape[0]
    order = jnp.concatenate([frame_pairs[:, 0], frame_pairs[-1:, 1]])
    chain = padded[order].reshape(pair_count + 1, line_count, 2, -1)
    front = chain[:-1]
    later = chain[1:]
    out_len = sample_rows + 4
    prod_len = out_len + WIN - 1
    xr = front[:, :, 0, WIN // 2 : WIN // 2 + prod_len]
    xi = front[:, :, 1, WIN // 2 : WIN // 2 + prod_len]
    yr = later[:, :, 0]
    yi = later[:, :, 1]
    nlag = 2 * MAXLAG + 1
    prods = jnp.stack(
        [xr * yr[..., j : j + prod_len] + xi * yi[..., j : j + prod_len] for j in range(nlag)]
    )
    cross_sum = window_sum(prods)
    power_a = window_sum(xr * xr + xi * xi) / (2 * WIN)
    ey = yr * yr + yi * yi
    power_full = window_sum(ey[..., : out_len + nlag - 1 + WIN - 1]) / (2 * WIN)
    root_b = jnp.sqrt(power_full + epsilon)
    root_a = 2 * WIN * jnp.sqrt(power_a + epsilon)

    own = jnp.repeat(lag_f, BLK, axis=2)
    peak_full = jnp.concatenate(
        [jnp.repeat(lag_prev, 2, axis=2), own, jnp.repeat(lag_next, 2, axis=2)], axis=2
    ).astype(jnp.int32)
    want = peak_full + MAXLAG
    best = None
    at_prev = jnp.zeros_like(root_a)
    centre = jnp.zeros_like(root_a)
    at_next = jnp.zeros_like(root_a)
    for j in range(nlag):
        score = cross_sum[j] / (root_a * root_b[..., j : j + out_len])
        best = score if best is None else jnp.maximum(best, score)
        at_prev = jnp.where(want == j + 1, score, at_prev)
        centre = jnp.where(want == j, score, centre)
        at_next = jnp.where(want == j - 1, score, at_next)
    quality = best[..., 2 : 2 + sample_rows]

    curvature = jnp.maximum(2.0 * centre - at_prev - at_next, 0.25)
    displacement = peak_full.astype(jnp.float32) + (at_next - at_prev) / (2.0 * curvature)
    zo = lax.broadcasted_iota(jnp.int32, displacement.shape, 2)
    outside = ((tile == 0) & (zo < 2)) | ((tile == tiles - 1) & (zo >= sample_rows + 2))
    dz = jnp.where(outside, 0.0, displacement)
    strain = (
        dz[..., 0:sample_rows]
        - 8.0 * dz[..., 1 : sample_rows + 1]
        + 8.0 * dz[..., 3 : sample_rows + 3]
        - dz[..., 4 : sample_rows + 4]
    ) / 12.0
    return (quality, strain)


def solution(mesh):
    chan = mesh.shape["chan"]
    tile = mesh.shape["tile"]
    devices = mesh.devices.reshape(chan // 4, 2, 2, tile)
    fine = Mesh(devices, CHAN + ("tile",))
    return jax.shard_map(
        shards,
        mesh=fine,
        in_specs=(
            P(None, "tile", CHAN),
            P("tile", None, CHAN, None),
            P(None, CHAN, "tile"),
            P(),
        ),
        out_specs=(P(None, CHAN, "tile"), P(None, CHAN, "tile")),
        check_vma=False,
    )
```

```python
import jax
import jax.numpy as jnp
from jax import lax
from jax.sharding import Mesh, PartitionSpec as P

MAXLAG = 16
WIN = 32
BLK = 8
HALO = MAXLAG + WIN // 2 + 2

epsilon = 1e-05

CHAN = ("cx", "cy", "cc")


def window_sum(values):
    width = 1
    while width < WIN:
        n = values.shape[-1] - width
        values = values[..., :n] + values[..., width : width + n]
        width *= 2
    return values


def from_left(block, axis):
    count = lax.axis_size(axis)
    return lax.ppermute(block, axis, [(i, i + 1) for i in range(count - 1)])


def from_right(block, axis):
    count = lax.axis_size(axis)
    return lax.ppermute(block, axis, [(i + 1, i) for i in range(count - 1)])


def beamform(extended, weights):
    return lax.conv_general_dilated(
        extended,
        weights,
        window_strides=(1,),
        padding="VALID",
        dimension_numbers=("NWC", "WIO", "NCW"),
        preferred_element_type=jnp.float32,
    )


def shards(channel_data, delay_weights, peak_lags, frame_pairs):
    frames, sample_rows, _ = channel_data.shape
    tap_count = delay_weights.shape[1]
    nx, ny, nc = (lax.axis_size(a) for a in CHAN)
    tile = lax.axis_index("tile")
    tiles = lax.axis_size("tile")

    lag_f = peak_lags.astype(jnp.float32)
    pairs_n, lines_n, _ = peak_lags.shape
    rim = channel_data[:, : tap_count - 1, :]
    rim_rows = from_right(rim, "tile")
    main_rows = sample_rows - tap_count + 1
    tail_rows = jnp.concatenate([channel_data[:, main_rows:, :], rim_rows], axis=1)

    weights = delay_weights[0]
    taps, cin, cols = weights.shape
    per_dev = cols // (nx * ny * nc)
    w6 = weights.reshape(taps, cin, nx, ny, nc, per_dev)
    core = lax.axis_index("cc")
    w_mine = lax.dynamic_index_in_dim(w6, core, 4, keepdims=False).reshape(taps, cin, -1)
    w_other = lax.dynamic_index_in_dim(w6, 1 - core, 4, keepdims=False).reshape(taps, cin, -1)
    def beam(w):
        return jnp.concatenate([beamform(channel_data, w), beamform(tail_rows, w)], axis=2)

    vol_other = beam(w_other)
    vol_mine = beam(w_mine)
    vol = vol_mine + lax.ppermute(vol_other, "cc", [(0, 1), (1, 0)])
    vol = vol.reshape(frames, nx * ny, per_dev, sample_rows)
    vol = lax.all_to_all(vol, ("cx", "cy"), 1, 1, tiled=True).sum(axis=1)

    head = vol[..., :HALO]
    tail = vol[..., sample_rows - HALO :]
    sent = jnp.concatenate([tail.reshape(-1), lag_f[:, :, -1].reshape(-1)])
    got = from_left(sent, "tile")
    left = got[: tail.size].reshape(tail.shape)
    lag_prev = got[tail.size :].reshape(pairs_n, lines_n, 1)
    sent = jnp.concatenate([head.reshape(-1), lag_f[:, :, 0].reshape(-1)])
    got = from_right(sent, "tile")
    right = got[: head.size].reshape(head.shape)
    lag_next = got[head.size :].reshape(pairs_n, lines_n, 1)
    padded = jnp.concatenate([left, vol, right], axis=2)

    line_count = per_dev // 2
    pair_count = frame_pairs.shape[0]
    order = jnp.concatenate([frame_pairs[:, 0], frame_pairs[-1:, 1]])
    chain = padded[order].reshape(pair_count + 1, line_count, 2, -1)
    front = chain[:-1]
    later = chain[1:]
    out_len = sample_rows + 4
    prod_len = out_len + WIN - 1
    xr = front[:, :, 0, WIN // 2 : WIN // 2 + prod_len]
    xi = front[:, :, 1, WIN // 2 : WIN // 2 + prod_len]
    yr = later[:, :, 0]
    yi = later[:, :, 1]
    nlag = 2 * MAXLAG + 1
    prods = jnp.stack(
        [xr * yr[..., j : j + prod_len] + xi * yi[..., j : j + prod_len] for j in range(nlag)]
    )
    cross_sum = window_sum(prods)
    power_a = window_sum(xr * xr + xi * xi) / (2 * WIN)
    ey = yr * yr + yi * yi
    power_full = window_sum(ey[..., : out_len + nlag - 1 + WIN - 1]) / (2 * WIN)
    root_b = jnp.sqrt(power_full + epsilon)
    root_a = 2 * WIN * jnp.sqrt(power_a + epsilon)

    own = jnp.repeat(lag_f, BLK, axis=2)
    peak_full = jnp.concatenate(
        [jnp.repeat(lag_prev, 2, axis=2), own, jnp.repeat(lag_next, 2, axis=2)], axis=2
    ).astype(jnp.int32)
    want = peak_full + MAXLAG
    best = None
    at_prev = jnp.zeros_like(root_a)
    centre = jnp.zeros_like(root_a)
    at_next = jnp.zeros_like(root_a)
    for j in range(nlag):
        score = cross_sum[j] / (root_a * root_b[..., j : j + out_len])
        best = score if best is None else jnp.maximum(best, score)
        at_prev = jnp.where(want == j + 1, score, at_prev)
        centre = jnp.where(want == j, score, centre)
        at_next = jnp.where(want == j - 1, score, at_next)
    quality = best[..., 2 : 2 + sample_rows]

    curvature = jnp.maximum(2.0 * centre - at_prev - at_next, 0.25)
    displacement = peak_full.astype(jnp.float32) + (at_next - at_prev) / (2.0 * curvature)
    zo = lax.broadcasted_iota(jnp.int32, displacement.shape, 2)
    outside = ((tile == 0) & (zo < 2)) | ((tile == tiles - 1) & (zo >= sample_rows + 2))
    dz = jnp.where(outside, 0.0, displacement)
    strain = (
        dz[..., 0:sample_rows]
        - 8.0 * dz[..., 1 : sample_rows + 1]
        + 8.0 * dz[..., 3 : sample_rows + 3]
        - dz[..., 4 : sample_rows + 4]
    ) / 12.0
    return (quality, strain)


def solution(mesh):
    chan = mesh.shape["chan"]
    tile = mesh.shape["tile"]
    devices = mesh.devices.reshape(chan // 4, 2, 2, tile)
    fine = Mesh(devices, CHAN + ("tile",))
    return jax.shard_map(
        shards,
        mesh=fine,
        in_specs=(
            P(None, "tile", CHAN),
            P("tile", None, CHAN, None),
            P(None, CHAN, "tile"),
            P(),
        ),
        out_specs=(P(None, CHAN, "tile"), P(None, CHAN, "tile")),
        check_vma=False,
    )
```

```python
import jax
import jax.numpy as jnp
from jax import lax
from jax.sharding import Mesh, PartitionSpec as P

MAXLAG = 16
WIN = 32
BLK = 8
HALO = MAXLAG + WIN // 2 + 2

epsilon = 1e-05

CHAN = ("cx", "cy", "cc")


def window_sum(values):
    width = 1
    while width < WIN:
        n = values.shape[-1] - width
        values = values[..., :n] + values[..., width : width + n]
        width *= 2
    return values


def from_left(block, axis):
    count = lax.axis_size(axis)
    return lax.ppermute(block, axis, [(i, i + 1) for i in range(count - 1)])


def from_right(block, axis):
    count = lax.axis_size(axis)
    return lax.ppermute(block, axis, [(i + 1, i) for i in range(count - 1)])


def beamform(extended, weights):
    return lax.conv_general_dilated(
        extended,
        weights,
        window_strides=(1,),
        padding="VALID",
        dimension_numbers=("NWC", "WIO", "NCW"),
        preferred_element_type=jnp.float32,
    )


def shards(channel_data, delay_weights, peak_lags, frame_pairs):
    frames, sample_rows, _ = channel_data.shape
    tap_count = delay_weights.shape[1]
    nx, ny, nc = (lax.axis_size(a) for a in CHAN)
    tile = lax.axis_index("tile")
    tiles = lax.axis_size("tile")

    lag_f = peak_lags.astype(jnp.float32)
    pairs_n, lines_n, _ = peak_lags.shape
    rim = channel_data[:, : tap_count - 1, :]
    first_lags = peak_lags[:, :, 0].astype(channel_data.dtype).reshape(-1)
    plane = rim.shape[1] * rim.shape[2]
    first_lags = jnp.pad(first_lags, (0, plane - first_lags.size)).reshape((1,) + rim.shape[1:])
    got = from_right(jnp.concatenate([rim, first_lags], axis=0), "tile")
    rim_rows = got[:frames]
    lag_next = got[frames].reshape(-1)[: pairs_n * lines_n].astype(jnp.float32)
    lag_next = lag_next.reshape(pairs_n, lines_n, 1)
    main_rows = sample_rows - tap_count + 1
    tail_rows = jnp.concatenate([channel_data[:, main_rows:, :], rim_rows], axis=1)

    weights = delay_weights[0]
    taps, cin, cols = weights.shape
    per_dev = cols // (nx * ny * nc)
    w6 = weights.reshape(taps, cin, nx, ny, nc, per_dev)
    core = lax.axis_index("cc")
    w_mine = lax.dynamic_index_in_dim(w6, core, 4, keepdims=False).reshape(taps, cin, -1)
    w_other = lax.dynamic_index_in_dim(w6, 1 - core, 4, keepdims=False).reshape(taps, cin, -1)
    def beam(w):
        return jnp.concatenate([beamform(channel_data, w), beamform(tail_rows, w)], axis=2)

    vol_other = beam(w_other)
    vol_mine = beam(w_mine)
    vol = vol_mine + lax.ppermute(vol_other, "cc", [(0, 1), (1, 0)])
    vol = vol.reshape(frames, nx * ny, per_dev, sample_rows)
    vol = lax.all_to_all(vol, ("cx", "cy"), 1, 1, tiled=True).sum(axis=1)

    head = vol[..., :HALO]
    tail = vol[..., sample_rows - HALO :]
    sent = jnp.concatenate([tail.reshape(-1), lag_f[:, :, -1].reshape(-1)])
    got = from_left(sent, "tile")
    left = got[: tail.size].reshape(tail.shape)
    lag_prev = got[tail.size :].reshape(pairs_n, lines_n, 1)
    padded = jnp.concatenate([left, vol, from_right(head, "tile")], axis=2)

    line_count = per_dev // 2
    pair_count = frame_pairs.shape[0]
    order = jnp.concatenate([frame_pairs[:, 0], frame_pairs[-1:, 1]])
    chain = padded[order].reshape(pair_count + 1, line_count, 2, -1)
    front = chain[:-1]
    later = chain[1:]
    out_len = sample_rows + 4
    prod_len = out_len + WIN - 1
    xr = front[:, :, 0, WIN // 2 : WIN // 2 + prod_len]
    xi = front[:, :, 1, WIN // 2 : WIN // 2 + prod_len]
    yr = later[:, :, 0]
    yi = later[:, :, 1]
    nlag = 2 * MAXLAG + 1
    prods = jnp.stack(
        [xr * yr[..., j : j + prod_len] + xi * yi[..., j : j + prod_len] for j in range(nlag)]
    )
    flat = prods.reshape(nlag, pair_count, line_count * prod_len)
    flat = jnp.pad(window_sum(flat), ((0, 0), (0, 0), (0, WIN - 1)))
    cross_sum = flat.reshape(nlag, pair_count, line_count, prod_len)[..., :out_len]
    power_a = window_sum(xr * xr + xi * xi) / (2 * WIN)
    ey = yr * yr + yi * yi
    power_full = window_sum(ey[..., : out_len + nlag - 1 + WIN - 1]) / (2 * WIN)
    root_b = jnp.sqrt(power_full + epsilon)
    root_a = 2 * WIN * jnp.sqrt(power_a + epsilon)

    own = jnp.repeat(lag_f, BLK, axis=2)
    peak_full = jnp.concatenate(
        [jnp.repeat(lag_prev, 2, axis=2), own, jnp.repeat(lag_next, 2, axis=2)], axis=2
    ).astype(jnp.int32)
    want = peak_full + MAXLAG
    best = None
    at_prev = jnp.zeros_like(root_a)
    centre = jnp.zeros_like(root_a)
    at_next = jnp.zeros_like(root_a)
    for j in range(nlag):
        score = cross_sum[j] / (root_a * root_b[..., j : j + out_len])
        best = score if best is None else jnp.maximum(best, score)
        at_prev = jnp.where(want == j + 1, score, at_prev)
        centre = jnp.where(want == j, score, centre)
        at_next = jnp.where(want == j - 1, score, at_next)
    quality = best[..., 2 : 2 + sample_rows]

    curvature = jnp.maximum(2.0 * centre - at_prev - at_next, 0.25)
    displacement = peak_full.astype(jnp.float32) + (at_next - at_prev) / (2.0 * curvature)
    zo = lax.broadcasted_iota(jnp.int32, displacement.shape, 2)
    outside = ((tile == 0) & (zo < 2)) | ((tile == tiles - 1) & (zo >= sample_rows + 2))
    dz = jnp.where(outside, 0.0, displacement)
    strain = (
        dz[..., 0:sample_rows]
        - 8.0 * dz[..., 1 : sample_rows + 1]
        + 8.0 * dz[..., 3 : sample_rows + 3]
        - dz[..., 4 : sample_rows + 4]
    ) / 12.0
    return (quality, strain)


def solution(mesh):
    chan = mesh.shape["chan"]
    tile = mesh.shape["tile"]
    devices = mesh.devices.reshape(chan // 4, 2, 2, tile)
    fine = Mesh(devices, CHAN + ("tile",))
    return jax.shard_map(
        shards,
        mesh=fine,
        in_specs=(
            P(None, "tile", CHAN),
            P("tile", None, CHAN, None),
            P(None, CHAN, "tile"),
            P(),
        ),
        out_specs=(P(None, CHAN, "tile"), P(None, CHAN, "tile")),
        check_vma=False,
    )
```

```python
import jax
import jax.numpy as jnp
from jax import lax
from jax.sharding import Mesh, PartitionSpec as P

MAXLAG = 16
WIN = 32
BLK = 8
HALO = MAXLAG + WIN // 2 + 2

epsilon = 1e-05

CHAN = ("cx", "cy", "cc")


def window_sum(values):
    width = 1
    while width < WIN:
        n = values.shape[-1] - width
        values = values[..., :n] + values[..., width : width + n]
        width *= 2
    return values


def from_left(block, axis):
    count = lax.axis_size(axis)
    return lax.ppermute(block, axis, [(i, i + 1) for i in range(count - 1)])


def from_right(block, axis):
    count = lax.axis_size(axis)
    return lax.ppermute(block, axis, [(i + 1, i) for i in range(count - 1)])


def beamform(extended, weights):
    return lax.conv_general_dilated(
        extended,
        weights,
        window_strides=(1,),
        padding="VALID",
        dimension_numbers=("NWC", "WIO", "NCW"),
        preferred_element_type=jnp.float32,
    )


def shards(channel_data, delay_weights, peak_lags, frame_pairs):
    frames, sample_rows, _ = channel_data.shape
    tap_count = delay_weights.shape[1]
    nx, ny, nc = (lax.axis_size(a) for a in CHAN)
    tile = lax.axis_index("tile")
    tiles = lax.axis_size("tile")

    lag_f = peak_lags.astype(jnp.float32)
    pairs_n, lines_n, _ = peak_lags.shape
    rim = channel_data[:, : tap_count - 1, :]
    first_lags = peak_lags[:, :, 0].astype(channel_data.dtype).reshape(-1)
    plane = rim.shape[1] * rim.shape[2]
    first_lags = jnp.pad(first_lags, (0, plane - first_lags.size)).reshape((1,) + rim.shape[1:])
    got = from_right(jnp.concatenate([rim, first_lags], axis=0), "tile")
    rim_rows = got[:frames]
    lag_next = got[frames].reshape(-1)[: pairs_n * lines_n].astype(jnp.float32)
    lag_next = lag_next.reshape(pairs_n, lines_n, 1)
    main_rows = sample_rows - tap_count + 1
    tail_rows = jnp.concatenate([channel_data[:, main_rows:, :], rim_rows], axis=1)

    weights = delay_weights[0]
    taps, cin, cols = weights.shape
    per_dev = cols // (nx * ny * nc)
    w6 = weights.reshape(taps, cin, nx, ny, nc, per_dev)
    core = lax.axis_index("cc")
    w_mine = lax.dynamic_index_in_dim(w6, core, 4, keepdims=False).reshape(taps, cin, -1)
    w_other = lax.dynamic_index_in_dim(w6, 1 - core, 4, keepdims=False).reshape(taps, cin, -1)
    def beam(w):
        return jnp.concatenate([beamform(channel_data, w), beamform(tail_rows, w)], axis=2)

    vol_other = beam(w_other)
    vol_mine = beam(w_mine)
    vol = vol_mine + lax.ppermute(vol_other, "cc", [(0, 1), (1, 0)])
    vol = vol.reshape(frames, nx * ny, per_dev, sample_rows)
    vol = lax.all_to_all(vol, ("cx", "cy"), 1, 1, tiled=True).sum(axis=1)

    head = vol[..., :HALO]
    tail = vol[..., sample_rows - HALO :]
    sent = jnp.concatenate([tail.reshape(-1), lag_f[:, :, -1].reshape(-1)])
    got = from_left(sent, "tile")
    left = got[: tail.size].reshape(tail.shape)
    lag_prev = got[tail.size :].reshape(pairs_n, lines_n, 1)
    padded = jnp.concatenate([left, vol, from_right(head, "tile")], axis=2)

    line_count = per_dev // 2
    pair_count = frame_pairs.shape[0]
    order = jnp.concatenate([frame_pairs[:, 0], frame_pairs[-1:, 1]])
    chain = padded[order].reshape(pair_count + 1, line_count, 2, -1)
    front = chain[:-1]
    later = chain[1:]
    out_len = sample_rows + 4
    prod_len = out_len + WIN - 1
    xr = front[:, :, 0, WIN // 2 : WIN // 2 + prod_len]
    xi = front[:, :, 1, WIN // 2 : WIN // 2 + prod_len]
    yr = later[:, :, 0]
    yi = later[:, :, 1]
    nlag = 2 * MAXLAG + 1
    group = 3

    def lag_group(first):
        lags = range(first, min(first + group, nlag))
        yr_g = jnp.stack([yr[..., j : j + prod_len] for j in lags])
        yi_g = jnp.stack([yi[..., j : j + prod_len] for j in lags])
        return xr[None] * yr_g + xi[None] * yi_g

    prods = jnp.concatenate([lag_group(first) for first in range(0, nlag, group)], axis=0)
    cross_sum = window_sum(prods)
    power_a = window_sum(xr * xr + xi * xi) / (2 * WIN)
    ey = yr * yr + yi * yi
    power_full = window_sum(ey[..., : out_len + nlag - 1 + WIN - 1]) / (2 * WIN)
    root_b = jnp.sqrt(power_full + epsilon)
    root_a = 2 * WIN * jnp.sqrt(power_a + epsilon)

    own = jnp.repeat(lag_f, BLK, axis=2)
    peak_full = jnp.concatenate(
        [jnp.repeat(lag_prev, 2, axis=2), own, jnp.repeat(lag_next, 2, axis=2)], axis=2
    ).astype(jnp.int32)
    want = peak_full + MAXLAG
    best = None
    at_prev = jnp.zeros_like(root_a)
    centre = jnp.zeros_like(root_a)
    at_next = jnp.zeros_like(root_a)
    for j in range(nlag):
        score = cross_sum[j] / (root_a * root_b[..., j : j + out_len])
        best = score if best is None else jnp.maximum(best, score)
        at_prev = jnp.where(want == j + 1, score, at_prev)
        centre = jnp.where(want == j, score, centre)
        at_next = jnp.where(want == j - 1, score, at_next)
    quality = best[..., 2 : 2 + sample_rows]

    curvature = jnp.maximum(2.0 * centre - at_prev - at_next, 0.25)
    displacement = peak_full.astype(jnp.float32) + (at_next - at_prev) / (2.0 * curvature)
    zo = lax.broadcasted_iota(jnp.int32, displacement.shape, 2)
    outside = ((tile == 0) & (zo < 2)) | ((tile == tiles - 1) & (zo >= sample_rows + 2))
    dz = jnp.where(outside, 0.0, displacement)
    strain = (
        dz[..., 0:sample_rows]
        - 8.0 * dz[..., 1 : sample_rows + 1]
        + 8.0 * dz[..., 3 : sample_rows + 3]
        - dz[..., 4 : sample_rows + 4]
    ) / 12.0
    return (quality, strain)


def solution(mesh):
    chan = mesh.shape["chan"]
    tile = mesh.shape["tile"]
    devices = mesh.devices.reshape(chan // 4, 2, 2, tile)
    fine = Mesh(devices, CHAN + ("tile",))
    return jax.shard_map(
        shards,
        mesh=fine,
        in_specs=(
            P(None, "tile", CHAN),
            P("tile", None, CHAN, None),
            P(None, CHAN, "tile"),
            P(),
        ),
        out_specs=(P(None, CHAN, "tile"), P(None, CHAN, "tile")),
        check_vma=False,
    )
```

```python
import jax
import jax.numpy as jnp
from jax import lax
from jax.sharding import Mesh, PartitionSpec as P

MAXLAG = 16
WIN = 32
BLK = 8
HALO = MAXLAG + WIN // 2 + 2

epsilon = 1e-05

CHAN = ("cx", "cy", "cc")


def window_sum(values):
    width = 1
    while width < WIN:
        n = values.shape[-1] - width
        values = values[..., :n] + values[..., width : width + n]
        width *= 2
    return values


def from_left(block, axis):
    count = lax.axis_size(axis)
    return lax.ppermute(block, axis, [(i, i + 1) for i in range(count - 1)])


def from_right(block, axis):
    count = lax.axis_size(axis)
    return lax.ppermute(block, axis, [(i + 1, i) for i in range(count - 1)])


def beamform(extended, weights):
    return lax.conv_general_dilated(
        extended,
        weights,
        window_strides=(1,),
        padding="VALID",
        dimension_numbers=("NWC", "WIO", "NCW"),
        preferred_element_type=jnp.float32,
    )


def shards(channel_data, delay_weights, peak_lags, frame_pairs):
    frames, sample_rows, _ = channel_data.shape
    tap_count = delay_weights.shape[1]
    nx, ny, nc = (lax.axis_size(a) for a in CHAN)
    tile = lax.axis_index("tile")
    tiles = lax.axis_size("tile")

    lag_f = peak_lags.astype(jnp.float32)
    pairs_n, lines_n, _ = peak_lags.shape
    rim = channel_data[:, : tap_count - 1, :]
    first_lags = peak_lags[:, :, 0].astype(channel_data.dtype).reshape(-1)
    plane = rim.shape[1] * rim.shape[2]
    first_lags = jnp.pad(first_lags, (0, plane - first_lags.size)).reshape((1,) + rim.shape[1:])
    got = from_right(jnp.concatenate([rim, first_lags], axis=0), "tile")
    rim_rows = got[:frames]
    lag_next = got[frames].reshape(-1)[: pairs_n * lines_n].astype(jnp.float32)
    lag_next = lag_next.reshape(pairs_n, lines_n, 1)
    main_rows = sample_rows - tap_count + 1
    tail_rows = jnp.concatenate([channel_data[:, main_rows:, :], rim_rows], axis=1)

    weights = delay_weights[0]
    taps, cin, cols = weights.shape
    per_dev = cols // (nx * ny * nc)
    w6 = weights.reshape(taps, cin, nx, ny, nc, per_dev)
    core = lax.axis_index("cc")
    w_mine = lax.dynamic_index_in_dim(w6, core, 4, keepdims=False).reshape(taps, cin, -1)
    w_other = lax.dynamic_index_in_dim(w6, 1 - core, 4, keepdims=False).reshape(taps, cin, -1)
    swap = [(0, 1), (1, 0)]
    got_main = lax.ppermute(beamform(channel_data, w_other), "cc", swap)
    got_tail = lax.ppermute(beamform(tail_rows, w_other), "cc", swap)
    vol_mine = jnp.concatenate([beamform(channel_data, w_mine), beamform(tail_rows, w_mine)], axis=2)
    vol = vol_mine + jnp.concatenate([got_main, got_tail], axis=2)
    vol = vol.reshape(frames, nx * ny, per_dev, sample_rows)
    vol = lax.all_to_all(vol, ("cx", "cy"), 1, 1, tiled=True).sum(axis=1)

    head = vol[..., :HALO]
    tail = vol[..., sample_rows - HALO :]
    sent = jnp.concatenate([tail.reshape(-1), lag_f[:, :, -1].reshape(-1)])
    got = from_left(sent, "tile")
    left = got[: tail.size].reshape(tail.shape)
    lag_prev = got[tail.size :].reshape(pairs_n, lines_n, 1)
    padded = jnp.concatenate([left, vol, from_right(head, "tile")], axis=2)

    line_count = per_dev // 2
    pair_count = frame_pairs.shape[0]
    order = jnp.concatenate([frame_pairs[:, 0], frame_pairs[-1:, 1]])
    chain = padded[order].reshape(pair_count + 1, line_count, 2, -1)
    front = chain[:-1]
    later = chain[1:]
    out_len = sample_rows + 4
    prod_len = out_len + WIN - 1
    xr = front[:, :, 0, WIN // 2 : WIN // 2 + prod_len]
    xi = front[:, :, 1, WIN // 2 : WIN // 2 + prod_len]
    yr = later[:, :, 0]
    yi = later[:, :, 1]
    nlag = 2 * MAXLAG + 1
    prods = jnp.stack(
        [xr * yr[..., j : j + prod_len] + xi * yi[..., j : j + prod_len] for j in range(nlag)]
    )
    cross_sum = window_sum(prods)
    power_a = window_sum(xr * xr + xi * xi) / (2 * WIN)
    ey = yr * yr + yi * yi
    power_full = window_sum(ey[..., : out_len + nlag - 1 + WIN - 1]) / (2 * WIN)
    root_b = jnp.sqrt(power_full + epsilon)
    root_a = 2 * WIN * jnp.sqrt(power_a + epsilon)

    own = jnp.repeat(lag_f, BLK, axis=2)
    peak_full = jnp.concatenate(
        [jnp.repeat(lag_prev, 2, axis=2), own, jnp.repeat(lag_next, 2, axis=2)], axis=2
    ).astype(jnp.int32)
    want = peak_full + MAXLAG
    best = None
    at_prev = jnp.zeros_like(root_a)
    centre = jnp.zeros_like(root_a)
    at_next = jnp.zeros_like(root_a)
    for j in range(nlag):
        score = cross_sum[j] / (root_a * root_b[..., j : j + out_len])
        best = score if best is None else jnp.maximum(best, score)
        at_prev = jnp.where(want == j + 1, score, at_prev)
        centre = jnp.where(want == j, score, centre)
        at_next = jnp.where(want == j - 1, score, at_next)
    quality = best[..., 2 : 2 + sample_rows]

    curvature = jnp.maximum(2.0 * centre - at_prev - at_next, 0.25)
    displacement = peak_full.astype(jnp.float32) + (at_next - at_prev) / (2.0 * curvature)
    zo = lax.broadcasted_iota(jnp.int32, displacement.shape, 2)
    outside = ((tile == 0) & (zo < 2)) | ((tile == tiles - 1) & (zo >= sample_rows + 2))
    dz = jnp.where(outside, 0.0, displacement)
    strain = (
        dz[..., 0:sample_rows]
        - 8.0 * dz[..., 1 : sample_rows + 1]
        + 8.0 * dz[..., 3 : sample_rows + 3]
        - dz[..., 4 : sample_rows + 4]
    ) / 12.0
    return (quality, strain)


def solution(mesh):
    chan = mesh.shape["chan"]
    tile = mesh.shape["tile"]
    devices = mesh.devices.reshape(chan // 4, 2, 2, tile)
    fine = Mesh(devices, CHAN + ("tile",))
    return jax.shard_map(
        shards,
        mesh=fine,
        in_specs=(
            P(None, "tile", CHAN),
            P("tile", None, CHAN, None),
            P(None, CHAN, "tile"),
            P(),
        ),
        out_specs=(P(None, CHAN, "tile"), P(None, CHAN, "tile")),
        check_vma=False,
    )
```

```python
import jax
import jax.numpy as jnp
from jax import lax
from jax.sharding import Mesh, PartitionSpec as P

MAXLAG = 16
WIN = 32
BLK = 8
HALO = MAXLAG + WIN // 2 + 2

epsilon = 1e-05

CHAN = ("cx", "cy", "cc")


def window_sum(values):
    width = 1
    while width < WIN:
        n = values.shape[-1] - width
        values = values[..., :n] + values[..., width : width + n]
        width *= 2
    return values


def from_left(block, axis):
    count = lax.axis_size(axis)
    return lax.ppermute(block, axis, [(i, i + 1) for i in range(count - 1)])


def from_right(block, axis):
    count = lax.axis_size(axis)
    return lax.ppermute(block, axis, [(i + 1, i) for i in range(count - 1)])


def beamform(extended, weights):
    return lax.conv_general_dilated(
        extended,
        weights,
        window_strides=(1,),
        padding="VALID",
        dimension_numbers=("NWC", "WIO", "NCW"),
        preferred_element_type=jnp.float32,
    )


def shards(channel_data, delay_weights, peak_lags, frame_pairs):
    frames, sample_rows, _ = channel_data.shape
    tap_count = delay_weights.shape[1]
    nx, ny, nc = (lax.axis_size(a) for a in CHAN)
    tile = lax.axis_index("tile")
    tiles = lax.axis_size("tile")

    lag_f = peak_lags.astype(jnp.float32)
    pairs_n, lines_n, _ = peak_lags.shape
    rim = channel_data[:, : tap_count - 1, :]
    first_lags = peak_lags[:, :, 0].astype(channel_data.dtype).reshape(-1)
    plane = rim.shape[1] * rim.shape[2]
    first_lags = jnp.pad(first_lags, (0, plane - first_lags.size)).reshape((1,) + rim.shape[1:])
    got = from_right(jnp.concatenate([rim, first_lags], axis=0), "tile")
    rim_rows = got[:frames]
    lag_next = got[frames].reshape(-1)[: pairs_n * lines_n].astype(jnp.float32)
    lag_next = lag_next.reshape(pairs_n, lines_n, 1)
    main_rows = sample_rows - tap_count + 1
    tail_rows = jnp.concatenate([channel_data[:, main_rows:, :], rim_rows], axis=1)

    weights = delay_weights[0]
    taps, cin, cols = weights.shape
    per_dev = cols // (nx * ny * nc)
    w6 = weights.reshape(taps, cin, nx, ny, nc, per_dev)
    core = lax.axis_index("cc")
    w_mine = lax.dynamic_index_in_dim(w6, core, 4, keepdims=False).reshape(taps, cin, -1)
    w_other = lax.dynamic_index_in_dim(w6, 1 - core, 4, keepdims=False).reshape(taps, cin, -1)
    def beam(w):
        return jnp.concatenate([beamform(channel_data, w), beamform(tail_rows, w)], axis=2)

    vol_other = beam(w_other)
    vol_mine = beam(w_mine)
    vol = vol_mine + lax.ppermute(vol_other, "cc", [(0, 1), (1, 0)])
    vol = vol.reshape(frames, nx * ny, per_dev, sample_rows)
    vol = lax.all_to_all(vol, ("cx", "cy"), 1, 1, tiled=True).sum(axis=1)

    head = vol[..., :HALO]
    tail = vol[..., sample_rows - HALO :]
    last_lags = lag_f[:, :, -1].reshape(-1)
    plane = tail.shape[1] * tail.shape[2]
    last_lags = jnp.pad(last_lags, (0, plane - last_lags.size)).reshape((1,) + tail.shape[1:])
    got = from_left(jnp.concatenate([tail, last_lags], axis=0), "tile")
    left = got[:frames]
    lag_prev = got[frames].reshape(-1)[: pairs_n * lines_n].reshape(pairs_n, lines_n, 1)
    padded = jnp.concatenate([left, vol, from_right(head, "tile")], axis=2)

    line_count = per_dev // 2
    pair_count = frame_pairs.shape[0]
    order = jnp.concatenate([frame_pairs[:, 0], frame_pairs[-1:, 1]])
    chain = padded[order].reshape(pair_count + 1, line_count, 2, -1)
    front = chain[:-1]
    later = chain[1:]
    out_len = sample_rows + 4
    prod_len = out_len + WIN - 1
    xr = front[:, :, 0, WIN // 2 : WIN // 2 + prod_len]
    xi = front[:, :, 1, WIN // 2 : WIN // 2 + prod_len]
    yr = later[:, :, 0]
    yi = later[:, :, 1]
    nlag = 2 * MAXLAG + 1
    prods = jnp.stack(
        [xr * yr[..., j : j + prod_len] + xi * yi[..., j : j + prod_len] for j in range(nlag)]
    )
    cross_sum = window_sum(prods)
    power_a = window_sum(xr * xr + xi * xi) / (2 * WIN)
    ey = yr * yr + yi * yi
    power_full = window_sum(ey[..., : out_len + nlag - 1 + WIN - 1]) / (2 * WIN)
    root_b = jnp.sqrt(power_full + epsilon)
    root_a = 2 * WIN * jnp.sqrt(power_a + epsilon)

    own = jnp.repeat(lag_f, BLK, axis=2)
    peak_full = jnp.concatenate(
        [jnp.repeat(lag_prev, 2, axis=2), own, jnp.repeat(lag_next, 2, axis=2)], axis=2
    ).astype(jnp.int32)
    want = peak_full + MAXLAG
    best = None
    at_prev = jnp.zeros_like(root_a)
    centre = jnp.zeros_like(root_a)
    at_next = jnp.zeros_like(root_a)
    for j in range(nlag):
        score = cross_sum[j] / (root_a * root_b[..., j : j + out_len])
        best = score if best is None else jnp.maximum(best, score)
        at_prev = jnp.where(want == j + 1, score, at_prev)
        centre = jnp.where(want == j, score, centre)
        at_next = jnp.where(want == j - 1, score, at_next)
    quality = best[..., 2 : 2 + sample_rows]

    curvature = jnp.maximum(2.0 * centre - at_prev - at_next, 0.25)
    displacement = peak_full.astype(jnp.float32) + (at_next - at_prev) / (2.0 * curvature)
    zo = lax.broadcasted_iota(jnp.int32, displacement.shape, 2)
    outside = ((tile == 0) & (zo < 2)) | ((tile == tiles - 1) & (zo >= sample_rows + 2))
    dz = jnp.where(outside, 0.0, displacement)
    strain = (
        dz[..., 0:sample_rows]
        - 8.0 * dz[..., 1 : sample_rows + 1]
        + 8.0 * dz[..., 3 : sample_rows + 3]
        - dz[..., 4 : sample_rows + 4]
    ) / 12.0
    return (quality, strain)


def solution(mesh):
    chan = mesh.shape["chan"]
    tile = mesh.shape["tile"]
    devices = mesh.devices.reshape(chan // 4, 2, 2, tile)
    fine = Mesh(devices, CHAN + ("tile",))
    return jax.shard_map(
        shards,
        mesh=fine,
        in_specs=(
            P(None, "tile", CHAN),
            P("tile", None, CHAN, None),
            P(None, CHAN, "tile"),
            P(),
        ),
        out_specs=(P(None, CHAN, "tile"), P(None, CHAN, "tile")),
        check_vma=False,
    )
```

```python
import jax
import jax.numpy as jnp
from jax import lax
from jax.sharding import Mesh, PartitionSpec as P

MAXLAG = 16
WIN = 32
BLK = 8
HALO = MAXLAG + WIN // 2 + 2

epsilon = 1e-05

CHAN = ("cx", "cy", "cc")


def window_sum(values):
    width = 1
    while width < WIN:
        n = values.shape[-1] - width
        values = values[..., :n] + values[..., width : width + n]
        width *= 2
    return values


def from_left(block, axis):
    count = lax.axis_size(axis)
    return lax.ppermute(block, axis, [(i, i + 1) for i in range(count - 1)])


def from_right(block, axis):
    count = lax.axis_size(axis)
    return lax.ppermute(block, axis, [(i + 1, i) for i in range(count - 1)])


def beamform(extended, weights):
    return lax.conv_general_dilated(
        extended,
        weights,
        window_strides=(1,),
        padding="VALID",
        dimension_numbers=("NWC", "WIO", "NCW"),
        preferred_element_type=jnp.float32,
    )


def shards(channel_data, delay_weights, peak_lags, frame_pairs):
    frames, sample_rows, _ = channel_data.shape
    tap_count = delay_weights.shape[1]
    nx, ny, nc = (lax.axis_size(a) for a in CHAN)
    tile = lax.axis_index("tile")
    tiles = lax.axis_size("tile")

    lag_f = peak_lags.astype(jnp.float32)
    pairs_n, lines_n, _ = peak_lags.shape
    rim = channel_data[:, : tap_count - 1, :]
    rim_rows = from_right(rim, "tile")
    main_rows = sample_rows - tap_count + 1
    tail_rows = jnp.concatenate([channel_data[:, main_rows:, :], rim_rows], axis=1)

    weights = delay_weights[0]
    taps, cin, cols = weights.shape
    per_dev = cols // (nx * ny * nc)
    w6 = weights.reshape(taps, cin, nx, ny, nc, per_dev)
    core = lax.axis_index("cc")
    w_mine = lax.dynamic_index_in_dim(w6, core, 4, keepdims=False).reshape(taps, cin, -1)
    w_other = lax.dynamic_index_in_dim(w6, 1 - core, 4, keepdims=False).reshape(taps, cin, -1)
    def beam(w):
        return jnp.concatenate([beamform(channel_data, w), beamform(tail_rows, w)], axis=2)

    vol_other = beam(w_other)
    vol_mine = beam(w_mine)
    vol = vol_mine + lax.ppermute(vol_other, "cc", [(0, 1), (1, 0)])
    vol = vol.reshape(frames, nx * ny, per_dev, sample_rows)
    vol = lax.all_to_all(vol, ("cx", "cy"), 1, 1, tiled=True).sum(axis=1)

    head = vol[..., :HALO]
    tail = vol[..., sample_rows - HALO :]
    last_lags = lag_f[:, :, -1].reshape(-1)
    plane = tail.shape[1] * tail.shape[2]
    last_lags = jnp.pad(last_lags, (0, plane - last_lags.size)).reshape((1,) + tail.shape[1:])
    got = from_left(jnp.concatenate([tail, last_lags], axis=0), "tile")
    left = got[:frames]
    lag_prev = got[frames].reshape(-1)[: pairs_n * lines_n].reshape(pairs_n, lines_n, 1)
    first_lags = lag_f[:, :, 0].reshape(-1)
    first_lags = jnp.pad(first_lags, (0, plane - first_lags.size)).reshape((1,) + head.shape[1:])
    got = from_right(jnp.concatenate([head, first_lags], axis=0), "tile")
    right = got[:frames]
    lag_next = got[frames].reshape(-1)[: pairs_n * lines_n].reshape(pairs_n, lines_n, 1)
    padded = jnp.concatenate([left, vol, right], axis=2)

    line_count = per_dev // 2
    pair_count = frame_pairs.shape[0]
    order = jnp.concatenate([frame_pairs[:, 0], frame_pairs[-1:, 1]])
    chain = padded[order].reshape(pair_count + 1, line_count, 2, -1)
    front = chain[:-1]
    later = chain[1:]
    out_len = sample_rows + 4
    prod_len = out_len + WIN - 1
    xr = front[:, :, 0, WIN // 2 : WIN // 2 + prod_len]
    xi = front[:, :, 1, WIN // 2 : WIN // 2 + prod_len]
    yr = later[:, :, 0]
    yi = later[:, :, 1]
    nlag = 2 * MAXLAG + 1
    prods = jnp.stack(
        [xr * yr[..., j : j + prod_len] + xi * yi[..., j : j + prod_len] for j in range(nlag)]
    )
    cross_sum = window_sum(prods)
    power_a = window_sum(xr * xr + xi * xi) / (2 * WIN)
    ey = yr * yr + yi * yi
    power_full = window_sum(ey[..., : out_len + nlag - 1 + WIN - 1]) / (2 * WIN)
    root_b = jnp.sqrt(power_full + epsilon)
    root_a = 2 * WIN * jnp.sqrt(power_a + epsilon)

    own = jnp.repeat(lag_f, BLK, axis=2)
    peak_full = jnp.concatenate(
        [jnp.repeat(lag_prev, 2, axis=2), own, jnp.repeat(lag_next, 2, axis=2)], axis=2
    ).astype(jnp.int32)
    want = peak_full + MAXLAG
    best = None
    at_prev = jnp.zeros_like(root_a)
    centre = jnp.zeros_like(root_a)
    at_next = jnp.zeros_like(root_a)
    for j in range(nlag):
        score = cross_sum[j] / (root_a * root_b[..., j : j + out_len])
        best = score if best is None else jnp.maximum(best, score)
        at_prev = jnp.where(want == j + 1, score, at_prev)
        centre = jnp.where(want == j, score, centre)
        at_next = jnp.where(want == j - 1, score, at_next)
    quality = best[..., 2 : 2 + sample_rows]

    curvature = jnp.maximum(2.0 * centre - at_prev - at_next, 0.25)
    displacement = peak_full.astype(jnp.float32) + (at_next - at_prev) / (2.0 * curvature)
    zo = lax.broadcasted_iota(jnp.int32, displacement.shape, 2)
    outside = ((tile == 0) & (zo < 2)) | ((tile == tiles - 1) & (zo >= sample_rows + 2))
    dz = jnp.where(outside, 0.0, displacement)
    strain = (
        dz[..., 0:sample_rows]
        - 8.0 * dz[..., 1 : sample_rows + 1]
        + 8.0 * dz[..., 3 : sample_rows + 3]
        - dz[..., 4 : sample_rows + 4]
    ) / 12.0
    return (quality, strain)


def solution(mesh):
    chan = mesh.shape["chan"]
    tile = mesh.shape["tile"]
    devices = mesh.devices.reshape(chan // 4, 2, 2, tile)
    fine = Mesh(devices, CHAN + ("tile",))
    return jax.shard_map(
        shards,
        mesh=fine,
        in_specs=(
            P(None, "tile", CHAN),
            P("tile", None, CHAN, None),
            P(None, CHAN, "tile"),
            P(),
        ),
        out_specs=(P(None, CHAN, "tile"), P(None, CHAN, "tile")),
        check_vma=False,
    )
```

```python
import jax
import jax.numpy as jnp
from jax import lax
from jax.sharding import Mesh, PartitionSpec as P

MAXLAG = 16
WIN = 32
BLK = 8
HALO = MAXLAG + WIN // 2 + 2

epsilon = 1e-05

CHAN = ("cx", "cy", "cc")


def window_sum(values):
    width = 1
    while width < WIN:
        n = values.shape[-1] - width
        values = values[..., :n] + values[..., width : width + n]
        width *= 2
    return values


def from_left(block, axis):
    count = lax.axis_size(axis)
    return lax.ppermute(block, axis, [(i, i + 1) for i in range(count - 1)])


def from_right(block, axis):
    count = lax.axis_size(axis)
    return lax.ppermute(block, axis, [(i + 1, i) for i in range(count - 1)])


def beamform(extended, weights):
    return lax.conv_general_dilated(
        extended,
        weights,
        window_strides=(1,),
        padding="VALID",
        dimension_numbers=("NWC", "WIO", "NCW"),
        preferred_element_type=jnp.float32,
    )


def shards(channel_data, delay_weights, peak_lags, frame_pairs):
    frames, sample_rows, _ = channel_data.shape
    tap_count = delay_weights.shape[1]
    nx, ny, nc = (lax.axis_size(a) for a in CHAN)
    tile = lax.axis_index("tile")
    tiles = lax.axis_size("tile")

    lag_f = peak_lags.astype(jnp.float32)
    pairs_n, lines_n, _ = peak_lags.shape
    rim = channel_data[:, :tap_count, :]
    first_lags = peak_lags[:, :, 0].astype(channel_data.dtype).reshape(-1)
    plane = rim.shape[1] * rim.shape[2]
    first_lags = jnp.pad(first_lags, (0, plane - first_lags.size)).reshape((1,) + rim.shape[1:])
    got = from_right(jnp.concatenate([rim, first_lags], axis=0), "tile")
    rim_rows = got[:frames]
    lag_next = got[frames].reshape(-1)[: pairs_n * lines_n].astype(jnp.float32)
    lag_next = lag_next.reshape(pairs_n, lines_n, 1)
    main_rows = sample_rows - tap_count + 1
    tail_rows = jnp.concatenate([channel_data[:, main_rows:, :], rim_rows[:, : tap_count - 1]], axis=1)

    weights = delay_weights[0]
    taps, cin, cols = weights.shape
    per_dev = cols // (nx * ny * nc)
    w6 = weights.reshape(taps, cin, nx, ny, nc, per_dev)
    core = lax.axis_index("cc")
    w_mine = lax.dynamic_index_in_dim(w6, core, 4, keepdims=False).reshape(taps, cin, -1)
    w_other = lax.dynamic_index_in_dim(w6, 1 - core, 4, keepdims=False).reshape(taps, cin, -1)
    def beam(w):
        return jnp.concatenate([beamform(channel_data, w), beamform(tail_rows, w)], axis=2)

    vol_other = beam(w_other)
    vol_mine = beam(w_mine)
    vol = vol_mine + lax.ppermute(vol_other, "cc", [(0, 1), (1, 0)])
    vol = vol.reshape(frames, nx * ny, per_dev, sample_rows)
    vol = lax.all_to_all(vol, ("cx", "cy"), 1, 1, tiled=True).sum(axis=1)

    head = vol[..., :HALO]
    tail = vol[..., sample_rows - HALO :]
    last_lags = lag_f[:, :, -1].reshape(-1)
    plane = tail.shape[1] * tail.shape[2]
    last_lags = jnp.pad(last_lags, (0, plane - last_lags.size)).reshape((1,) + tail.shape[1:])
    got = from_left(jnp.concatenate([tail, last_lags], axis=0), "tile")
    left = got[:frames]
    lag_prev = got[frames].reshape(-1)[: pairs_n * lines_n].reshape(pairs_n, lines_n, 1)
    padded = jnp.concatenate([left, vol, from_right(head, "tile")], axis=2)

    line_count = per_dev // 2
    pair_count = frame_pairs.shape[0]
    order = jnp.concatenate([frame_pairs[:, 0], frame_pairs[-1:, 1]])
    chain = padded[order].reshape(pair_count + 1, line_count, 2, -1)
    front = chain[:-1]
    later = chain[1:]
    out_len = sample_rows + 4
    prod_len = out_len + WIN - 1
    xr = front[:, :, 0, WIN // 2 : WIN // 2 + prod_len]
    xi = front[:, :, 1, WIN // 2 : WIN // 2 + prod_len]
    yr = later[:, :, 0]
    yi = later[:, :, 1]
    nlag = 2 * MAXLAG + 1
    prods = jnp.stack(
        [xr * yr[..., j : j + prod_len] + xi * yi[..., j : j + prod_len] for j in range(nlag)]
    )
    cross_sum = window_sum(prods)
    power_a = window_sum(xr * xr + xi * xi) / (2 * WIN)
    ey = yr * yr + yi * yi
    power_full = window_sum(ey[..., : out_len + nlag - 1 + WIN - 1]) / (2 * WIN)
    root_b = jnp.sqrt(power_full + epsilon)
    root_a = 2 * WIN * jnp.sqrt(power_a + epsilon)

    own = jnp.repeat(lag_f, BLK, axis=2)
    peak_full = jnp.concatenate(
        [jnp.repeat(lag_prev, 2, axis=2), own, jnp.repeat(lag_next, 2, axis=2)], axis=2
    ).astype(jnp.int32)
    want = peak_full + MAXLAG
    best = None
    at_prev = jnp.zeros_like(root_a)
    centre = jnp.zeros_like(root_a)
    at_next = jnp.zeros_like(root_a)
    for j in range(nlag):
        score = cross_sum[j] / (root_a * root_b[..., j : j + out_len])
        best = score if best is None else jnp.maximum(best, score)
        at_prev = jnp.where(want == j + 1, score, at_prev)
        centre = jnp.where(want == j, score, centre)
        at_next = jnp.where(want == j - 1, score, at_next)
    quality = best[..., 2 : 2 + sample_rows]

    curvature = jnp.maximum(2.0 * centre - at_prev - at_next, 0.25)
    displacement = peak_full.astype(jnp.float32) + (at_next - at_prev) / (2.0 * curvature)
    zo = lax.broadcasted_iota(jnp.int32, displacement.shape, 2)
    outside = ((tile == 0) & (zo < 2)) | ((tile == tiles - 1) & (zo >= sample_rows + 2))
    dz = jnp.where(outside, 0.0, displacement)
    strain = (
        dz[..., 0:sample_rows]
        - 8.0 * dz[..., 1 : sample_rows + 1]
        + 8.0 * dz[..., 3 : sample_rows + 3]
        - dz[..., 4 : sample_rows + 4]
    ) / 12.0
    return (quality, strain)


def solution(mesh):
    chan = mesh.shape["chan"]
    tile = mesh.shape["tile"]
    devices = mesh.devices.reshape(chan // 4, 2, 2, tile)
    fine = Mesh(devices, CHAN + ("tile",))
    return jax.shard_map(
        shards,
        mesh=fine,
        in_specs=(
            P(None, "tile", CHAN),
            P("tile", None, CHAN, None),
            P(None, CHAN, "tile"),
            P(),
        ),
        out_specs=(P(None, CHAN, "tile"), P(None, CHAN, "tile")),
        check_vma=False,
    )
```

```python
import jax
import jax.numpy as jnp
from jax import lax
from jax.sharding import Mesh, PartitionSpec as P

MAXLAG = 16
WIN = 32
BLK = 8
HALO = MAXLAG + WIN // 2 + 2

epsilon = 1e-05

CHAN = ("cx", "cy", "cc")


def window_sum(values):
    width = 1
    while width < WIN:
        n = values.shape[-1] - width
        values = values[..., :n] + values[..., width : width + n]
        width *= 2
    return values


def from_left(block, axis):
    count = lax.axis_size(axis)
    return lax.ppermute(block, axis, [(i, i + 1) for i in range(count - 1)])


def from_right(block, axis):
    count = lax.axis_size(axis)
    return lax.ppermute(block, axis, [(i + 1, i) for i in range(count - 1)])


def beamform(extended, weights):
    return lax.conv_general_dilated(
        extended,
        weights,
        window_strides=(1,),
        padding="VALID",
        dimension_numbers=("NWC", "WIO", "NCW"),
        preferred_element_type=jnp.float32,
    )


def shards(channel_data, delay_weights, peak_lags, frame_pairs):
    frames, sample_rows, _ = channel_data.shape
    tap_count = delay_weights.shape[1]
    nx, ny, nc = (lax.axis_size(a) for a in CHAN)
    tile = lax.axis_index("tile")
    tiles = lax.axis_size("tile")

    lag_f = peak_lags.astype(jnp.float32)
    pairs_n, lines_n, _ = peak_lags.shape
    rim = channel_data[:, : tap_count - 1, :]
    first_lags = peak_lags[:, :, 0].astype(channel_data.dtype).reshape(-1)
    plane = rim.shape[1] * rim.shape[2]
    first_lags = jnp.pad(first_lags, (0, plane - first_lags.size)).reshape((1,) + rim.shape[1:])
    got = from_right(jnp.concatenate([rim, first_lags], axis=0), "tile")
    rim_rows = got[:frames]
    lag_next = got[frames].reshape(-1)[: pairs_n * lines_n].astype(jnp.float32)
    lag_next = lag_next.reshape(pairs_n, lines_n, 1)
    main_rows = sample_rows - tap_count + 1
    tail_rows = jnp.concatenate([channel_data[:, main_rows:, :], rim_rows], axis=1)

    weights = delay_weights[0]
    taps, cin, cols = weights.shape
    per_dev = cols // (nx * ny * nc)
    w6 = weights.reshape(taps, cin, nx, ny, nc, per_dev)
    core = lax.axis_index("cc")
    w_mine = lax.dynamic_index_in_dim(w6, core, 4, keepdims=False).reshape(taps, cin, -1)
    w_other = lax.dynamic_index_in_dim(w6, 1 - core, 4, keepdims=False).reshape(taps, cin, -1)
    def beam(w):
        return jnp.concatenate([beamform(channel_data, w), beamform(tail_rows, w)], axis=2)

    vol_other = beam(w_other)
    vol_mine = beam(w_mine)
    vol = vol_mine + lax.ppermute(vol_other, "cc", [(0, 1), (1, 0)])
    vol = vol.reshape(frames, nx * ny, per_dev, sample_rows)
    vol = lax.all_to_all(vol, ("cx", "cy"), 1, 1, tiled=True).sum(axis=1)

    head = vol[..., :HALO]
    tail = vol[..., sample_rows - HALO :]
    last_lags = lag_f[:, :, -1].reshape(-1)
    plane = tail.shape[1] * tail.shape[2]
    last_lags = jnp.pad(last_lags, (0, plane - last_lags.size)).reshape((1,) + tail.shape[1:])
    got = from_left(jnp.concatenate([tail, last_lags], axis=0), "tile")
    left = got[:frames]
    lag_prev = got[frames].reshape(-1)[: pairs_n * lines_n].reshape(pairs_n, lines_n, 1)
    padded = jnp.concatenate([left, vol, from_right(head, "tile")], axis=2)

    line_count = per_dev // 2
    pair_count = frame_pairs.shape[0]
    order = jnp.concatenate([frame_pairs[:, 0], frame_pairs[-1:, 1]])
    chain = padded[order].reshape(pair_count + 1, line_count, 2, -1)
    front = chain[:-1]
    later = chain[1:]
    out_len = sample_rows + 4
    prod_len = out_len + WIN - 1
    xr = front[:, :, 0, WIN // 2 : WIN // 2 + prod_len]
    xi = front[:, :, 1, WIN // 2 : WIN // 2 + prod_len]
    yr = later[:, :, 0]
    yi = later[:, :, 1]
    nlag = 2 * MAXLAG + 1
    prods = jnp.stack(
        [xr * yr[..., j : j + prod_len] + xi * yi[..., j : j + prod_len] for j in range(nlag)]
    )
    cross_sum = window_sum(prods)
    energy = window_sum(chain[:, :, 0] * chain[:, :, 0] + chain[:, :, 1] * chain[:, :, 1]) / (2 * WIN)
    power_a = energy[:-1, :, WIN // 2 : WIN // 2 + out_len]
    power_full = energy[1:, :, : out_len + nlag - 1]
    root_b = jnp.sqrt(power_full + epsilon)
    root_a = 2 * WIN * jnp.sqrt(power_a + epsilon)

    own = jnp.repeat(lag_f, BLK, axis=2)
    peak_full = jnp.concatenate(
        [jnp.repeat(lag_prev, 2, axis=2), own, jnp.repeat(lag_next, 2, axis=2)], axis=2
    ).astype(jnp.int32)
    want = peak_full + MAXLAG
    best = None
    at_prev = jnp.zeros_like(root_a)
    centre = jnp.zeros_like(root_a)
    at_next = jnp.zeros_like(root_a)
    for j in range(nlag):
        score = cross_sum[j] / (root_a * root_b[..., j : j + out_len])
        best = score if best is None else jnp.maximum(best, score)
        at_prev = jnp.where(want == j + 1, score, at_prev)
        centre = jnp.where(want == j, score, centre)
        at_next = jnp.where(want == j - 1, score, at_next)
    quality = best[..., 2 : 2 + sample_rows]

    curvature = jnp.maximum(2.0 * centre - at_prev - at_next, 0.25)
    displacement = peak_full.astype(jnp.float32) + (at_next - at_prev) / (2.0 * curvature)
    zo = lax.broadcasted_iota(jnp.int32, displacement.shape, 2)
    outside = ((tile == 0) & (zo < 2)) | ((tile == tiles - 1) & (zo >= sample_rows + 2))
    dz = jnp.where(outside, 0.0, displacement)
    strain = (
        dz[..., 0:sample_rows]
        - 8.0 * dz[..., 1 : sample_rows + 1]
        + 8.0 * dz[..., 3 : sample_rows + 3]
        - dz[..., 4 : sample_rows + 4]
    ) / 12.0
    return (quality, strain)


def solution(mesh):
    chan = mesh.shape["chan"]
    tile = mesh.shape["tile"]
    devices = mesh.devices.reshape(chan // 4, 2, 2, tile)
    fine = Mesh(devices, CHAN + ("tile",))
    return jax.shard_map(
        shards,
        mesh=fine,
        in_specs=(
            P(None, "tile", CHAN),
            P("tile", None, CHAN, None),
            P(None, CHAN, "tile"),
            P(),
        ),
        out_specs=(P(None, CHAN, "tile"), P(None, CHAN, "tile")),
        check_vma=False,
    )
```
